32 devices in a mesh: dp: 8 (over z, y), tensor: 4 (over x, core).
Axes of the slice: x: 2, y: 2, z: 4, core: 2. Of those that a mesh axis runs over, the one named last changes fastest.
Arguments:
- up_inputs: bfloat16 [16384, 1024], P('dp'), may hold values from -6 to 6
- up_grad_out: bfloat16 [16384, 2816], P('dp', 'tensor'), may hold values from -0.125 to 0.125
- emb_ids: int32 [16384], P('dp'), may hold values from 0 to 4095
- emb_grad_out: bfloat16 [16384, 1024], P('dp', 'tensor'), may hold values from -6 to 6
- up_error: float32 [8, 1024, 2816], P('dp', None, 'tensor'), may hold values from -6 to 6
- emb_error: float32 [8, 4096, 1024], P('dp', None, 'tensor'), may hold values from -6 to 6
- up_moment: float32 [1024, 2816], P('dp', 'tensor'), may hold values from -2 to 2
- emb_moment: float32 [4096, 1024], P('dp', 'tensor'), may hold values from -2 to 2
- up_start: float32 [2816, 32], P('tensor'), may hold values from -0.109375 to 0.109375
- emb_start: float32 [1024, 32], P('tensor'), may hold values from -0.1875 to 0.1875
- up_gram_inv: float32 [2, 32, 32], replicated, may hold values from -2 to 3, as said below
- emb_gram_inv: float32 [2, 32, 32], replicated, may hold values from -2 to 3, as said below
- norm_grads: float32 [8, 2, 1024], P('dp'), may hold values from -6 to 6
- norm_moment: float32 [2, 1024], replicated, may hold values from -2 to 2
Outputs:
- up_error_new: float32 [8, 1024, 2816], P('dp', None, 'tensor')
- emb_error_new: float32 [8, 4096, 1024], P('dp', None, 'tensor')
- up_moment_new: float32 [1024, 2816], P('dp', 'tensor')
- emb_moment_new: float32 [4096, 1024], P('dp', 'tensor')
- up_step: bfloat16 [1024, 2816], P(None, 'tensor')
- emb_step: bfloat16 [4096, 1024], P(None, 'tensor')
- norm_moment_new: float32 [2, 1024], replicated
- norm_step: float32 [2, 1024], replicated
The draws below stay inside these ranges and needn't reach their ends.
Inputs may be any that keep to these rules, and one draw needn't show every extreme that they name: `up_gram_inv`: inverse Gram factor of each power round. `emb_gram_inv`: inverse Gram factor of each power round.
All inputs are finite; a program needn't handle non-finite values.
Results may differ from the reference program's by a relative error of at most 0.001.
Values may be sent and summed in bfloat16 or wider, within the bound.
No kernel may reach another device: no remote copies, remote signals or barrier semaphores. Data moves between devices by JAX's collectives and lax.ppermute only.
A program may use at most 128 MiB of HBM per device.

```python
import math
import jax
import jax.numpy as jnp
import numpy as np
from jax import lax

D = 1024
FF = 2816
V = 4096
R = 32
ROUNDS = 2
TOK = 2048
TOKENS = 16384
N_DP = 8


def gram_factor(key):
    first, second = jax.random.split(key)
    diag = jax.random.uniform(first, (ROUNDS, R), jnp.float32, 2.0, 3.0)
    off = jax.random.uniform(second, (ROUNDS, R, R), jnp.float32, -1.0, 1.0)
    eye = jnp.eye(R, dtype=jnp.float32)
    return eye * diag[:, :, None] + off * (1.5 / R) * (1.0 - eye)


def draw_up_gram_inv(key, part):
    return gram_factor(jax.random.fold_in(key, 31))


def draw_emb_gram_inv(key, part):
    return gram_factor(jax.random.fold_in(key, 57))


def touch_ends(array, rng, least, high):
    longest = array.shape.index(max(array.shape))
    spots = []
    for shift in (0, 1):
        where = [jax.random.randint(jax.random.fold_in(rng, axis), (), 0, length) for axis, length in enumerate(array.shape)]
        where[longest] = (where[longest] + shift) % array.shape[longest]
        spots.append(tuple(where))
    return array.at[spots[0]].set(least).at[spots[1]].set(high)


def levels(key, extent, cuts, smallest, largest):
    def one(position, shards_of):
        draws = jax.random.uniform(jax.random.fold_in(jax.random.fold_in(key, 6), position), (shards_of,), jnp.float32, smallest / len(cuts), largest / len(cuts))
        return jnp.repeat(jnp.exp(draws), extent[position] // shards_of).reshape((-1,) + (1,) * (len(extent) - position - 1))

    factor_of = one(*cuts[0])
    for cut in cuts[1:]:
        factor_of = factor_of * one(*cut)
    return factor_of


def cumulative_ranks(amount, skew):
    weights = [(1 << 20) // math.isqrt(grade ** skew) + 1 for grade in range(1, amount + 1)]
    width = 1 + sum(weights) // (1 << 30)
    return np.cumsum(np.array([max(1, weight // width) for weight in weights]))


def ranked_ids(own_key, dims, number_of, skew):
    table = cumulative_ranks(number_of, skew)
    ticket = jax.random.randint(jax.random.fold_in(own_key, 1), dims, 0, int(table[number_of - 1]))
    standing = jnp.searchsorted(jnp.asarray(table, jnp.int32), ticket, side="right")
    return jax.random.permutation(jax.random.fold_in(own_key, 2), number_of)[standing].astype(jnp.int32)


def noise(stream_key, dims, deviation, bound, pieces=(), held_as=jnp.bfloat16):
    loudness = levels(stream_key, dims, pieces, -0.22, 0.18) if pieces else 1.0
    drawn = jax.random.normal(stream_key, dims, jnp.float32) * deviation * loudness
    return jnp.minimum(jnp.maximum(drawn, -bound), bound).astype(held_as)


def setup_inputs(seed: int = 0) -> dict:
    arg_keys = jax.random.split(jax.random.key(seed), 15)
    up_inputs = noise(arg_keys[0], (TOKENS, D), 1.0, 6.0, ((0, 8),))
    up_grad_out = noise(arg_keys[1], (TOKENS, FF), TOK ** -0.5, 0.125, ((0, 8), (1, 4)))
    emb_ids = touch_ends(ranked_ids(arg_keys[2], (TOKENS,), V, 2), jax.random.fold_in(arg_keys[2], 3), 0, V - 1).astype(jnp.int32)
    emb_grad_out = noise(arg_keys[3], (TOKENS, D), 1.0, 6.0, ((0, 8), (1, 4)))
    up_error = noise(arg_keys[4], (N_DP, D, FF), 1.0, 6.0, ((0, 8), (2, 4)), jnp.float32)
    emb_error = noise(arg_keys[5], (N_DP, V, D), 1.0, 6.0, ((0, 8), (2, 4)), jnp.float32)
    up_moment = noise(arg_keys[6], (D, FF), 0.15, 2.0, ((0, 8), (1, 4)), jnp.float32)
    emb_moment = noise(arg_keys[7], (V, D), 0.15, 2.0, ((0, 8), (1, 4)), jnp.float32)
    up_start = noise(arg_keys[8], (FF, R), FF ** -0.5, 0.109375, ((0, 4),), jnp.float32)
    emb_start = noise(arg_keys[9], (D, R), D ** -0.5, 0.1875, ((0, 4),), jnp.float32)
    up_gram_inv = draw_up_gram_inv(jax.random.fold_in(arg_keys[14], 71), 0)
    emb_gram_inv = draw_emb_gram_inv(jax.random.fold_in(arg_keys[14], 71), 0)
    norm_grads = noise(arg_keys[12], (N_DP, 2, D), 1.0, 6.0, ((0, 8),), jnp.float32)
    norm_moment = noise(arg_keys[13], (2, D), 0.15, 2.0, (), jnp.float32)
    return dict(up_inputs=up_inputs, up_grad_out=up_grad_out, emb_ids=emb_ids, emb_grad_out=emb_grad_out, up_error=up_error, emb_error=emb_error, up_moment=up_moment, emb_moment=emb_moment, up_start=up_start, emb_start=emb_start, up_gram_inv=up_gram_inv, emb_gram_inv=emb_gram_inv, norm_grads=norm_grads, norm_moment=norm_moment)


BETA = 0.9

def normalized(left_sum, gram, rows):
    scale = lax.rsqrt(jnp.mean(left_sum * left_sum) + 1e-06) / math.sqrt(rows)
    return jnp.dot(left_sum, gram, precision=lax.Precision.HIGHEST) * scale

def power_rounds(field, right, gram_all, rows):
    left = None
    for step in range(ROUNDS):
        left_sum = jnp.einsum('rij,jk->ik', field, right, precision=lax.Precision.HIGHEST)
        left = normalized(left_sum, gram_all[step], rows)
        right = jnp.einsum('rij,ik->jk', field, left, precision=lax.Precision.HIGHEST)
    return jnp.dot(left, right.T, precision=lax.Precision.HIGHEST) / N_DP

def reference(up_inputs, up_grad_out, emb_ids, emb_grad_out, up_error, emb_error, up_moment, emb_moment, up_start, emb_start, up_gram_inv, emb_gram_inv, norm_grads, norm_moment):
    inputs_f = up_inputs.astype(jnp.float32).reshape(N_DP, TOK, D)
    grads_f = up_grad_out.astype(jnp.float32).reshape(N_DP, TOK, FF)
    up_field = jnp.einsum('rtd,rtf->rdf', inputs_f, grads_f, precision=lax.Precision.HIGHEST) + up_error
    offsets = (jnp.arange(N_DP, dtype=jnp.int32) * V)[:, None]
    segment = (emb_ids.reshape(N_DP, TOK) + offsets).reshape(-1)
    emb_terms = jax.ops.segment_sum(emb_grad_out.astype(jnp.float32), segment, num_segments=N_DP * V)
    emb_field = emb_terms.reshape(N_DP, V, D) + emb_error
    up_approx = power_rounds(up_field, up_start, up_gram_inv, D)
    emb_approx = power_rounds(emb_field, emb_start, emb_gram_inv, V)
    up_error_new = up_field - up_approx[None]
    emb_error_new = emb_field - emb_approx[None]
    up_moment_new = BETA * up_moment + up_approx
    emb_moment_new = BETA * emb_moment + emb_approx
    up_step = (up_approx + BETA * up_moment_new).astype(jnp.bfloat16)
    emb_step = (emb_approx + BETA * emb_moment_new).astype(jnp.bfloat16)
    norm_mean = lax.optimization_barrier(jnp.sum(norm_grads, axis=0)) / N_DP
    norm_moment_new = BETA * norm_moment + norm_mean
    norm_step = norm_mean + BETA * norm_moment_new
    return (up_error_new, emb_error_new, up_moment_new, emb_moment_new, up_step, emb_step, norm_moment_new, norm_step)
```

```python
import math

import jax
import jax.numpy as jnp
from jax import lax
from jax.sharding import PartitionSpec as P

BETA = 0.9
HIGHEST = lax.Precision.HIGHEST
ALL = ("dp", "tensor")


def log2_of(n):
    bits = n.bit_length() - 1
    assert 1 << bits == n
    return bits


def partner(bit, n):
    return [(i, i ^ (1 << bit)) for i in range(n)]


def doubling_sum(x, axes, n):
    for bit in range(log2_of(n)):
        x = x + lax.ppermute(x, axes, partner(bit, n))
    return x


def split_axis(shape):
    rows, lanes = shape
    if lanes % 256 == 0:
        return 1
    if rows % 16 == 0:
        return 0
    return 1 if lanes % 2 == 0 else 0


def halving_sum(x, axes, n, index):
    plan = []
    for bit in range(log2_of(n)):
        axis = split_axis(x.shape)
        half = x.shape[axis] // 2
        low = lax.slice_in_dim(x, 0, half, axis=axis)
        high = lax.slice_in_dim(x, half, 2 * half, axis=axis)
        upper = ((index >> bit) & 1) == 1
        keep = jnp.where(upper, high, low)
        send = jnp.where(upper, low, high)
        x = keep + lax.ppermute(send, axes, partner(bit, n))
        plan.append((bit, axis, upper))
    for bit, axis, upper in reversed(plan):
        got = lax.ppermute(x, axes, partner(bit, n))
        x = jnp.where(
            upper, jnp.concatenate([got, x], axis), jnp.concatenate([x, got], axis)
        )
    return x


def scale_of(left_sum_t, rows):
    return lax.rsqrt(jnp.mean(left_sum_t * left_sum_t) + 1e-06) / math.sqrt(rows)


def normalized_t(left_sum_t, gram, rows):
    out = lax.dot_general(gram, left_sum_t, (((0,), (0,)), ((), ())), precision=HIGHEST)
    return out * scale_of(left_sum_t, rows)


def left_t(field, right_t):
    return lax.dot_general(right_t, field, (((1,), (1,)), ((), ())), precision=HIGHEST)


def right_t(field, left_t_):
    return lax.dot_general(left_t_, field, (((1,), (0,)), ((), ())), precision=HIGHEST)


def outer_t(left_t_, right_t_):
    return lax.dot_general(left_t_, right_t_, (((0,), (0,)), ((), ())), precision=HIGHEST)


def per_device(
    up_inputs,
    up_grad_out,
    emb_ids,
    emb_grad_out,
    up_error,
    emb_error,
    up_moment,
    emb_moment,
    up_start,
    emb_start,
    up_gram_inv,
    emb_gram_inv,
    norm_grads,
    norm_moment,
):
    replicas = lax.axis_size("dp")
    tensors = lax.axis_size("tensor")
    world = replicas * tensors
    dp_index = lax.axis_index("dp")
    index = dp_index * tensors + lax.axis_index("tensor")

    up_moment_all = lax.all_gather(up_moment, "dp", axis=0, tiled=True)
    emb_moment_all = lax.all_gather(emb_moment, "dp", axis=0, tiled=True)

    up_field = (
        lax.dot_general(
            up_inputs, up_grad_out, (((0,), (0,)), ((), ())), preferred_element_type=jnp.float32
        )
        + up_error[0]
    )
    one_hot_rows = jax.nn.one_hot(emb_ids, emb_error.shape[1], dtype=jnp.bfloat16)
    emb_terms = lax.dot_general(
        one_hot_rows, emb_grad_out, (((0,), (0,)), ((), ())), preferred_element_type=jnp.float32
    )
    emb_field = emb_terms + emb_error[0]
    up_rows, up_cols = up_field.shape
    emb_rows, emb_cols = emb_field.shape

    norm_flat = norm_grads[0].reshape(1, -1)
    norm_len = norm_flat.shape[1]

    up_right = up_start.T
    emb_right = emb_start.T
    up_left = emb_left = None
    norm_total = None
    for step in range(up_gram_inv.shape[0]):
        parts = jnp.concatenate([left_t(up_field, up_right), left_t(emb_field, emb_right)], 1)
        sums = halving_sum(parts, ALL, world, index)
        up_left = normalized_t(sums[:, :up_rows], up_gram_inv[step], up_rows)
        emb_left = normalized_t(sums[:, up_rows:], emb_gram_inv[step], emb_rows)
        pieces = [right_t(up_field, up_left), right_t(emb_field, emb_left)]
        if step == 0:
            pad = -norm_len % up_right.shape[0]
            pieces.append(jnp.pad(norm_flat, ((0, 0), (0, pad))).reshape(up_right.shape[0], -1))
        sums = doubling_sum(jnp.concatenate(pieces, 1), "dp", replicas)
        up_right = sums[:, :up_cols]
        emb_right = sums[:, up_cols : up_cols + emb_cols]
        if step == 0:
            norm_total = sums[:, up_cols + emb_cols :].reshape(1, -1)[:, :norm_len]
            norm_total = norm_total.reshape(norm_grads.shape[1:])

    up_approx = outer_t(up_left, up_right) / replicas
    emb_approx = outer_t(emb_left, emb_right) / replicas
    up_error_new = (up_field - up_approx)[None]
    emb_error_new = (emb_field - emb_approx)[None]
    up_moment_all_new = BETA * up_moment_all + up_approx
    emb_moment_all_new = BETA * emb_moment_all + emb_approx
    up_step = (up_approx + BETA * up_moment_all_new).astype(jnp.bfloat16)
    emb_step = (emb_approx + BETA * emb_moment_all_new).astype(jnp.bfloat16)
    up_count = up_moment.shape[0]
    emb_count = emb_moment.shape[0]
    up_moment_new = lax.dynamic_slice_in_dim(up_moment_all_new, dp_index * up_count, up_count, 0)
    emb_moment_new = lax.dynamic_slice_in_dim(
        emb_moment_all_new, dp_index * emb_count, emb_count, 0
    )
    norm_mean = norm_total / replicas
    norm_moment_new = BETA * norm_moment + norm_mean
    norm_step = norm_mean + BETA * norm_moment_new
    return (
        up_error_new,
        emb_error_new,
        up_moment_new,
        emb_moment_new,
        up_step,
        emb_step,
        norm_moment_new,
        norm_step,
    )


def solution(mesh):
    return jax.shard_map(
        per_device,
        mesh=mesh,
        in_specs=(
            P("dp", None),
            P("dp", "tensor"),
            P("dp"),
            P("dp", "tensor"),
            P("dp", None, "tensor"),
            P("dp", None, "tensor"),
            P("dp", "tensor"),
            P("dp", "tensor"),
            P("tensor", None),
            P("tensor", None),
            P(),
            P(),
            P("dp", None, None),
            P(),
        ),
        out_specs=(
            P("dp", None, "tensor"),
            P("dp", None, "tensor"),
            P("dp", "tensor"),
            P("dp", "tensor"),
            P(None, "tensor"),
            P(None, "tensor"),
            P(),
            P(),
        ),
        check_vma=False,
    )
```

```python
import math

import jax
import jax.numpy as jnp
from jax import lax
from jax.sharding import PartitionSpec as P

BETA = 0.9
HIGHEST = lax.Precision.HIGHEST
HIGH = lax.Precision.HIGH
ALL = ("dp", "tensor")


def log2_of(n):
    bits = n.bit_length() - 1
    assert 1 << bits == n
    return bits


def partner(bit, n):
    return [(i, i ^ (1 << bit)) for i in range(n)]


def doubling_sum(x, axes, n):
    for bit in range(log2_of(n)):
        x = x + lax.ppermute(x, axes, partner(bit, n))
    return x


def split_axis(shape):
    rows, lanes = shape
    if lanes % 256 == 0:
        return 1
    if rows % 16 == 0:
        return 0
    return 1 if lanes % 2 == 0 else 0


def halving_sum(x, axes, n, index):
    plan = []
    for bit in range(log2_of(n)):
        axis = split_axis(x.shape)
        half = x.shape[axis] // 2
        low = lax.slice_in_dim(x, 0, half, axis=axis)
        high = lax.slice_in_dim(x, half, 2 * half, axis=axis)
        upper = ((index >> bit) & 1) == 1
        keep = jnp.where(upper, high, low)
        send = jnp.where(upper, low, high)
        x = keep + lax.ppermute(send, axes, partner(bit, n))
        plan.append((bit, axis, upper))
    for bit, axis, upper in reversed(plan):
        got = lax.ppermute(x, axes, partner(bit, n))
        x = jnp.where(
            upper, jnp.concatenate([got, x], axis), jnp.concatenate([x, got], axis)
        )
    return x


def scale_of(left_sum_t, rows):
    return lax.rsqrt(jnp.mean(left_sum_t * left_sum_t) + 1e-06) / math.sqrt(rows)


def normalized_t(left_sum_t, gram, rows):
    out = lax.dot_general(gram, left_sum_t, (((0,), (0,)), ((), ())), precision=HIGHEST)
    return out * scale_of(left_sum_t, rows)


def left_t(field, right_t):
    return lax.dot_general(right_t, field, (((1,), (1,)), ((), ())), precision=HIGH)


def right_t(field, left_t_):
    return lax.dot_general(left_t_, field, (((1,), (0,)), ((), ())), precision=HIGH)


def outer_t(left_t_, right_t_):
    return lax.dot_general(left_t_, right_t_, (((0,), (0,)), ((), ())), precision=HIGH)


def per_device(
    up_inputs,
    up_grad_out,
    emb_ids,
    emb_grad_out,
    up_error,
    emb_error,
    up_moment,
    emb_moment,
    up_start,
    emb_start,
    up_gram_inv,
    emb_gram_inv,
    norm_grads,
    norm_moment,
):
    replicas = lax.axis_size("dp")
    tensors = lax.axis_size("tensor")
    world = replicas * tensors
    dp_index = lax.axis_index("dp")
    index = dp_index * tensors + lax.axis_index("tensor")

    up_moment_all = lax.all_gather(up_moment, "dp", axis=0, tiled=True)
    emb_moment_all = lax.all_gather(emb_moment, "dp", axis=0, tiled=True)

    up_field = (
        lax.dot_general(
            up_inputs, up_grad_out, (((0,), (0,)), ((), ())), preferred_element_type=jnp.float32
        )
        + up_error[0]
    )
    one_hot_rows = jax.nn.one_hot(emb_ids, emb_error.shape[1], dtype=jnp.bfloat16)
    emb_terms = lax.dot_general(
        one_hot_rows, emb_grad_out, (((0,), (0,)), ((), ())), preferred_element_type=jnp.float32
    )
    emb_field = emb_terms + emb_error[0]
    up_rows, up_cols = up_field.shape
    emb_rows, emb_cols = emb_field.shape

    norm_flat = norm_grads[0].reshape(1, -1)
    norm_len = norm_flat.shape[1]

    up_right = up_start.T
    emb_right = emb_start.T
    up_left = emb_left = None
    norm_total = None
    for step in range(up_gram_inv.shape[0]):
        parts = jnp.concatenate([left_t(up_field, up_right), left_t(emb_field, emb_right)], 1)
        sums = halving_sum(parts, ALL, world, index)
        up_left = normalized_t(sums[:, :up_rows], up_gram_inv[step], up_rows)
        emb_left = normalized_t(sums[:, up_rows:], emb_gram_inv[step], emb_rows)
        pieces = [right_t(up_field, up_left), right_t(emb_field, emb_left)]
        if step == 0:
            pad = -norm_len % up_right.shape[0]
            pieces.append(jnp.pad(norm_flat, ((0, 0), (0, pad))).reshape(up_right.shape[0], -1))
        sums = doubling_sum(jnp.concatenate(pieces, 1), "dp", replicas)
        up_right = sums[:, :up_cols]
        emb_right = sums[:, up_cols : up_cols + emb_cols]
        if step == 0:
            norm_total = sums[:, up_cols + emb_cols :].reshape(1, -1)[:, :norm_len]
            norm_total = norm_total.reshape(norm_grads.shape[1:])

    up_approx = outer_t(up_left, up_right) / replicas
    emb_approx = outer_t(emb_left, emb_right) / replicas
    up_error_new = (up_field - up_approx)[None]
    emb_error_new = (emb_field - emb_approx)[None]
    up_moment_all_new = BETA * up_moment_all + up_approx
    emb_moment_all_new = BETA * emb_moment_all + emb_approx
    up_step = (up_approx + BETA * up_moment_all_new).astype(jnp.bfloat16)
    emb_step = (emb_approx + BETA * emb_moment_all_new).astype(jnp.bfloat16)
    up_count = up_moment.shape[0]
    emb_count = emb_moment.shape[0]
    up_moment_new = lax.dynamic_slice_in_dim(up_moment_all_new, dp_index * up_count, up_count, 0)
    emb_moment_new = lax.dynamic_slice_in_dim(
        emb_moment_all_new, dp_index * emb_count, emb_count, 0
    )
    norm_mean = norm_total / replicas
    norm_moment_new = BETA * norm_moment + norm_mean
    norm_step = norm_mean + BETA * norm_moment_new
    return (
        up_error_new,
        emb_error_new,
        up_moment_new,
        emb_moment_new,
        up_step,
        emb_step,
        norm_moment_new,
        norm_step,
    )


def solution(mesh):
    return jax.shard_map(
        per_device,
        mesh=mesh,
        in_specs=(
            P("dp", None),
            P("dp", "tensor"),
            P("dp"),
            P("dp", "tensor"),
            P("dp", None, "tensor"),
            P("dp", None, "tensor"),
            P("dp", "tensor"),
            P("dp", "tensor"),
            P("tensor", None),
            P("tensor", None),
            P(),
            P(),
            P("dp", None, None),
            P(),
        ),
        out_specs=(
            P("dp", None, "tensor"),
            P("dp", None, "tensor"),
            P("dp", "tensor"),
            P("dp", "tensor"),
            P(None, "tensor"),
            P(None, "tensor"),
            P(),
            P(),
        ),
        check_vma=False,
    )
```

```python
import math

import jax
import jax.numpy as jnp
from jax import lax
from jax.sharding import PartitionSpec as P

BETA = 0.9
HIGHEST = lax.Precision.HIGHEST
HIGH = lax.Precision.HIGH
ALL = ("dp", "tensor")


def log2_of(n):
    bits = n.bit_length() - 1
    assert 1 << bits == n
    return bits


def partner(bit, n):
    return [(i, i ^ (1 << bit)) for i in range(n)]


def doubling_sum(x, axes, n):
    for bit in range(log2_of(n)):
        x = x + lax.ppermute(x, axes, partner(bit, n))
    return x


def split_axis(shape):
    rows, lanes = shape
    if lanes % 256 == 0:
        return 1
    if rows % 16 == 0:
        return 0
    return 1 if lanes % 2 == 0 else 0


def halving_sum(x, axes, n, index, middle=None):
    plan = []
    for bit in range(log2_of(n)):
        axis = split_axis(x.shape)
        half = x.shape[axis] // 2
        low = lax.slice_in_dim(x, 0, half, axis=axis)
        high = lax.slice_in_dim(x, half, 2 * half, axis=axis)
        upper = ((index >> bit) & 1) == 1
        keep = jnp.where(upper, high, low)
        send = jnp.where(upper, low, high)
        x = keep + lax.ppermute(send, axes, partner(bit, n))
        plan.append((bit, axis, upper))
    if middle is not None:
        x = middle(x)
    for bit, axis, upper in reversed(plan):
        got = lax.ppermute(x, axes, partner(bit, n))
        x = jnp.where(
            upper, jnp.concatenate([got, x], axis), jnp.concatenate([x, got], axis)
        )
    return x


def scale_of(left_sum_t, rows):
    return lax.rsqrt(jnp.mean(left_sum_t * left_sum_t) + 1e-06) / math.sqrt(rows)


def normalized_t(left_sum_t, gram, rows):
    out = lax.dot_general(gram, left_sum_t, (((0,), (0,)), ((), ())), precision=HIGHEST)
    return out * scale_of(left_sum_t, rows)


def left_t(field, right_t):
    return lax.dot_general(right_t, field, (((1,), (1,)), ((), ())), precision=HIGH)


def right_t(field, left_t_):
    return lax.dot_general(left_t_, field, (((1,), (0,)), ((), ())), precision=HIGH)


def outer_t(left_t_, right_t_):
    return lax.dot_general(left_t_, right_t_, (((0,), (0,)), ((), ())), precision=HIGH)


def per_device(
    up_inputs,
    up_grad_out,
    emb_ids,
    emb_grad_out,
    up_error,
    emb_error,
    up_moment,
    emb_moment,
    up_start,
    emb_start,
    up_gram_inv,
    emb_gram_inv,
    norm_grads,
    norm_moment,
):
    replicas = lax.axis_size("dp")
    tensors = lax.axis_size("tensor")
    dp_index = lax.axis_index("dp")

    up_moment_all = lax.all_gather(up_moment, "dp", axis=0, tiled=True)
    emb_moment_all = lax.all_gather(emb_moment, "dp", axis=0, tiled=True)

    up_field = (
        lax.dot_general(
            up_inputs, up_grad_out, (((0,), (0,)), ((), ())), preferred_element_type=jnp.float32
        )
        + up_error[0]
    )
    one_hot_rows = jax.nn.one_hot(emb_ids, emb_error.shape[1], dtype=jnp.bfloat16)
    emb_terms = lax.dot_general(
        one_hot_rows, emb_grad_out, (((0,), (0,)), ((), ())), preferred_element_type=jnp.float32
    )
    emb_field = emb_terms + emb_error[0]
    up_rows, up_cols = up_field.shape
    emb_rows, emb_cols = emb_field.shape

    norm_flat = norm_grads[0].reshape(1, -1)
    norm_len = norm_flat.shape[1]

    up_right = up_start.T
    emb_right = emb_start.T
    up_left = emb_left = None
    norm_total = None
    for step in range(up_gram_inv.shape[0]):
        parts = jnp.concatenate([left_t(up_field, up_right), left_t(emb_field, emb_right)], 1)
        sums = halving_sum(
            parts,
            "tensor",
            tensors,
            lax.axis_index("tensor"),
            lambda chunk: doubling_sum(chunk, "dp", replicas),
        )
        up_left = normalized_t(sums[:, :up_rows], up_gram_inv[step], up_rows)
        emb_left = normalized_t(sums[:, up_rows:], emb_gram_inv[step], emb_rows)
        pieces = [right_t(up_field, up_left), right_t(emb_field, emb_left)]
        if step == 0:
            pad = -norm_len % up_right.shape[0]
            pieces.append(jnp.pad(norm_flat, ((0, 0), (0, pad))).reshape(up_right.shape[0], -1))
        sums = doubling_sum(jnp.concatenate(pieces, 1), "dp", replicas)
        up_right = sums[:, :up_cols]
        emb_right = sums[:, up_cols : up_cols + emb_cols]
        if step == 0:
            norm_total = sums[:, up_cols + emb_cols :].reshape(1, -1)[:, :norm_len]
            norm_total = norm_total.reshape(norm_grads.shape[1:])

    up_approx = outer_t(up_left, up_right) / replicas
    emb_approx = outer_t(emb_left, emb_right) / replicas
    up_error_new = (up_field - up_approx)[None]
    emb_error_new = (emb_field - emb_approx)[None]
    up_moment_all_new = BETA * up_moment_all + up_approx
    emb_moment_all_new = BETA * emb_moment_all + emb_approx
    up_step = (up_approx + BETA * up_moment_all_new).astype(jnp.bfloat16)
    emb_step = (emb_approx + BETA * emb_moment_all_new).astype(jnp.bfloat16)
    up_count = up_moment.shape[0]
    emb_count = emb_moment.shape[0]
    up_moment_new = lax.dynamic_slice_in_dim(up_moment_all_new, dp_index * up_count, up_count, 0)
    emb_moment_new = lax.dynamic_slice_in_dim(
        emb_moment_all_new, dp_index * emb_count, emb_count, 0
    )
    norm_mean = norm_total / replicas
    norm_moment_new = BETA * norm_moment + norm_mean
    norm_step = norm_mean + BETA * norm_moment_new
    return (
        up_error_new,
        emb_error_new,
        up_moment_new,
        emb_moment_new,
        up_step,
        emb_step,
        norm_moment_new,
        norm_step,
    )


def solution(mesh):
    return jax.shard_map(
        per_device,
        mesh=mesh,
        in_specs=(
            P("dp", None),
            P("dp", "tensor"),
            P("dp"),
            P("dp", "tensor"),
            P("dp", None, "tensor"),
            P("dp", None, "tensor"),
            P("dp", "tensor"),
            P("dp", "tensor"),
            P("tensor", None),
            P("tensor", None),
            P(),
            P(),
            P("dp", None, None),
            P(),
        ),
        out_specs=(
            P("dp", None, "tensor"),
            P("dp", None, "tensor"),
            P("dp", "tensor"),
            P("dp", "tensor"),
            P(None, "tensor"),
            P(None, "tensor"),
            P(),
            P(),
        ),
        check_vma=False,
    )
```

```python
import math

import jax
import jax.numpy as jnp
from jax import lax
from jax.sharding import PartitionSpec as P

BETA = 0.9
HIGHEST = lax.Precision.HIGHEST
HIGH = lax.Precision.HIGH
ALL = ("dp", "tensor")


def log2_of(n):
    bits = n.bit_length() - 1
    assert 1 << bits == n
    return bits


def partner(bit, n):
    return [(i, i ^ (1 << bit)) for i in range(n)]


def doubling_sum(x, axes, n):
    for bit in range(log2_of(n)):
        x = x + lax.ppermute(x, axes, partner(bit, n))
    return x


def split_axis(shape):
    rows, lanes = shape
    if lanes % 256 == 0:
        return 1
    if rows % 16 == 0:
        return 0
    return 1 if lanes % 2 == 0 else 0


def halving_sum(x, axes, n, index, middle=None):
    plan = []
    for bit in range(log2_of(n)):
        axis = split_axis(x.shape)
        half = x.shape[axis] // 2
        low = lax.slice_in_dim(x, 0, half, axis=axis)
        high = lax.slice_in_dim(x, half, 2 * half, axis=axis)
        upper = ((index >> bit) & 1) == 1
        keep = jnp.where(upper, high, low)
        send = jnp.where(upper, low, high)
        x = keep + lax.ppermute(send, axes, partner(bit, n))
        plan.append((bit, axis, upper))
    if middle is not None:
        x = middle(x)
    for bit, axis, upper in reversed(plan):
        got = lax.ppermute(x, axes, partner(bit, n))
        x = jnp.where(
            upper, jnp.concatenate([got, x], axis), jnp.concatenate([x, got], axis)
        )
    return x


def scale_of(left_sum_t, rows):
    return lax.rsqrt(jnp.mean(left_sum_t * left_sum_t) + 1e-06) / math.sqrt(rows)


def normalized_t(left_sum_t, gram, rows):
    out = lax.dot_general(gram, left_sum_t, (((0,), (0,)), ((), ())), precision=HIGHEST)
    return out * scale_of(left_sum_t, rows)


def left_t(field, right_t):
    return lax.dot_general(right_t, field, (((1,), (1,)), ((), ())), precision=HIGH)


def right_t(field, left_t_):
    return lax.dot_general(left_t_, field, (((1,), (0,)), ((), ())), precision=HIGH)


def outer_t(left_t_, right_t_):
    return lax.dot_general(left_t_, right_t_, (((0,), (0,)), ((), ())), precision=HIGH)


def per_device(
    up_inputs,
    up_grad_out,
    emb_ids,
    emb_grad_out,
    up_error,
    emb_error,
    up_moment,
    emb_moment,
    up_start,
    emb_start,
    up_gram_inv,
    emb_gram_inv,
    norm_grads,
    norm_moment,
):
    replicas = lax.axis_size("dp")
    tensors = lax.axis_size("tensor")
    dp_index = lax.axis_index("dp")

    up_moment_all = lax.all_gather(up_moment, "dp", axis=0, tiled=True)
    emb_moment_all = lax.all_gather(emb_moment, "dp", axis=0, tiled=True)

    up_field = (
        lax.dot_general(
            up_inputs, up_grad_out, (((0,), (0,)), ((), ())), preferred_element_type=jnp.float32
        )
        + up_error[0]
    )
    one_hot_rows = jax.nn.one_hot(emb_ids, emb_error.shape[1], dtype=jnp.bfloat16)
    emb_terms = lax.dot_general(
        one_hot_rows, emb_grad_out, (((0,), (0,)), ((), ())), preferred_element_type=jnp.float32
    )
    emb_field = emb_terms + emb_error[0]
    up_rows, up_cols = up_field.shape
    emb_rows, emb_cols = emb_field.shape

    norm_flat = norm_grads[0].reshape(1, -1)
    norm_len = norm_flat.shape[1]

    up_right = up_start.T
    emb_right = emb_start.T
    up_left = emb_left = None
    norm_total = None
    for step in range(up_gram_inv.shape[0]):
        if step == 0:
            up_part = left_t(up_inputs.T, left_t(up_grad_out, up_right)) + left_t(
                up_error[0], up_right
            )
            emb_part = left_t(one_hot_rows.T, left_t(emb_grad_out, emb_right)) + left_t(
                emb_error[0], emb_right
            )
        else:
            up_part = left_t(up_field, up_right)
            emb_part = left_t(emb_field, emb_right)
        parts = jnp.concatenate([up_part, emb_part], 1)
        sums = halving_sum(
            parts,
            "tensor",
            tensors,
            lax.axis_index("tensor"),
            lambda chunk: doubling_sum(chunk, "dp", replicas),
        )
        up_left = normalized_t(sums[:, :up_rows], up_gram_inv[step], up_rows)
        emb_left = normalized_t(sums[:, up_rows:], emb_gram_inv[step], emb_rows)
        pieces = [right_t(up_field, up_left), right_t(emb_field, emb_left)]
        if step == 0:
            pad = -norm_len % up_right.shape[0]
            pieces.append(jnp.pad(norm_flat, ((0, 0), (0, pad))).reshape(up_right.shape[0], -1))
        sums = doubling_sum(jnp.concatenate(pieces, 1), "dp", replicas)
        up_right = sums[:, :up_cols]
        emb_right = sums[:, up_cols : up_cols + emb_cols]
        if step == 0:
            norm_total = sums[:, up_cols + emb_cols :].reshape(1, -1)[:, :norm_len]
            norm_total = norm_total.reshape(norm_grads.shape[1:])

    up_approx = outer_t(up_left, up_right) / replicas
    emb_approx = outer_t(emb_left, emb_right) / replicas
    up_error_new = (up_field - up_approx)[None]
    emb_error_new = (emb_field - emb_approx)[None]
    up_moment_all_new = BETA * up_moment_all + up_approx
    emb_moment_all_new = BETA * emb_moment_all + emb_approx
    up_step = (up_approx + BETA * up_moment_all_new).astype(jnp.bfloat16)
    emb_step = (emb_approx + BETA * emb_moment_all_new).astype(jnp.bfloat16)
    up_count = up_moment.shape[0]
    emb_count = emb_moment.shape[0]
    up_moment_new = lax.dynamic_slice_in_dim(up_moment_all_new, dp_index * up_count, up_count, 0)
    emb_moment_new = lax.dynamic_slice_in_dim(
        emb_moment_all_new, dp_index * emb_count, emb_count, 0
    )
    norm_mean = norm_total / replicas
    norm_moment_new = BETA * norm_moment + norm_mean
    norm_step = norm_mean + BETA * norm_moment_new
    return (
        up_error_new,
        emb_error_new,
        up_moment_new,
        emb_moment_new,
        up_step,
        emb_step,
        norm_moment_new,
        norm_step,
    )


def solution(mesh):
    return jax.shard_map(
        per_device,
        mesh=mesh,
        in_specs=(
            P("dp", None),
            P("dp", "tensor"),
            P("dp"),
            P("dp", "tensor"),
            P("dp", None, "tensor"),
            P("dp", None, "tensor"),
            P("dp", "tensor"),
            P("dp", "tensor"),
            P("tensor", None),
            P("tensor", None),
            P(),
            P(),
            P("dp", None, None),
            P(),
        ),
        out_specs=(
            P("dp", None, "tensor"),
            P("dp", None, "tensor"),
            P("dp", "tensor"),
            P("dp", "tensor"),
            P(None, "tensor"),
            P(None, "tensor"),
            P(),
            P(),
        ),
        check_vma=False,
    )
```

```python
import math

import jax
import jax.numpy as jnp
from jax import lax
from jax.sharding import PartitionSpec as P

BETA = 0.9
HIGHEST = lax.Precision.HIGHEST
HIGH = lax.Precision.HIGH
ALL = ("dp", "tensor")


def log2_of(n):
    bits = n.bit_length() - 1
    assert 1 << bits == n
    return bits


def partner(bit, n):
    return [(i, i ^ (1 << bit)) for i in range(n)]


def doubling_sum(x, axes, n):
    for bit in range(log2_of(n)):
        x = x + lax.ppermute(x, axes, partner(bit, n))
    return x


def split_axis(shape):
    rows, lanes = shape
    if lanes % 256 == 0:
        return 1
    if rows % 16 == 0:
        return 0
    return 1 if lanes % 2 == 0 else 0


def halving_sum(x, axes, n, index, middle=None):
    plan = []
    for bit in range(log2_of(n)):
        axis = split_axis(x.shape)
        half = x.shape[axis] // 2
        low = lax.slice_in_dim(x, 0, half, axis=axis)
        high = lax.slice_in_dim(x, half, 2 * half, axis=axis)
        upper = ((index >> bit) & 1) == 1
        keep = jnp.where(upper, high, low)
        send = jnp.where(upper, low, high)
        x = keep + lax.ppermute(send, axes, partner(bit, n))
        plan.append((bit, axis, upper))
    if middle is not None:
        x = middle(x)
    for bit, axis, upper in reversed(plan):
        got = lax.ppermute(x, axes, partner(bit, n))
        x = jnp.where(
            upper, jnp.concatenate([got, x], axis), jnp.concatenate([x, got], axis)
        )
    return x


def scale_of(left_sum_t, rows):
    return lax.rsqrt(jnp.mean(left_sum_t * left_sum_t) + 1e-06) / math.sqrt(rows)


def normalized_t(left_sum_t, gram, rows):
    out = lax.dot_general(gram, left_sum_t, (((0,), (0,)), ((), ())), precision=HIGHEST)
    return out * scale_of(left_sum_t, rows)


def left_t(field, right_t):
    return lax.dot_general(right_t, field, (((1,), (1,)), ((), ())), precision=HIGH)


def right_t(field, left_t_):
    return lax.dot_general(left_t_, field, (((1,), (0,)), ((), ())), precision=HIGH)


def outer_t(left_t_, right_t_):
    return lax.dot_general(left_t_, right_t_, (((0,), (0,)), ((), ())), precision=HIGH)


def per_device(
    up_inputs,
    up_grad_out,
    emb_ids,
    emb_grad_out,
    up_error,
    emb_error,
    up_moment,
    emb_moment,
    up_start,
    emb_start,
    up_gram_inv,
    emb_gram_inv,
    norm_grads,
    norm_moment,
):
    replicas = lax.axis_size("dp")
    tensors = lax.axis_size("tensor")
    dp_index = lax.axis_index("dp")

    up_moment_all = lax.all_gather(up_moment, "dp", axis=0, tiled=True)
    emb_moment_all = lax.all_gather(emb_moment, "dp", axis=0, tiled=True)

    up_field = (
        lax.dot_general(
            up_inputs, up_grad_out, (((0,), (0,)), ((), ())), preferred_element_type=jnp.float32
        )
        + up_error[0]
    )
    vocab = emb_error.shape[1]
    one_hot_cols = (
        lax.broadcasted_iota(jnp.int32, (vocab, emb_ids.shape[0]), 0) == emb_ids[None, :]
    ).astype(jnp.bfloat16)
    emb_terms = lax.dot_general(
        one_hot_cols, emb_grad_out, (((1,), (0,)), ((), ())), preferred_element_type=jnp.float32
    )
    emb_field = emb_terms + emb_error[0]
    up_rows, up_cols = up_field.shape
    emb_rows, emb_cols = emb_field.shape

    norm_flat = norm_grads[0].reshape(1, -1)
    norm_len = norm_flat.shape[1]

    up_right = up_start.T
    emb_right = emb_start.T
    up_left = emb_left = None
    norm_total = None
    for step in range(up_gram_inv.shape[0]):
        parts = jnp.concatenate([left_t(up_field, up_right), left_t(emb_field, emb_right)], 1)
        sums = halving_sum(
            parts,
            "tensor",
            tensors,
            lax.axis_index("tensor"),
            lambda chunk: doubling_sum(chunk, "dp", replicas),
        )
        up_left = normalized_t(sums[:, :up_rows], up_gram_inv[step], up_rows)
        emb_left = normalized_t(sums[:, up_rows:], emb_gram_inv[step], emb_rows)
        pieces = [right_t(up_field, up_left), right_t(emb_field, emb_left)]
        if step == 0:
            pad = -norm_len % up_right.shape[0]
            pieces.append(jnp.pad(norm_flat, ((0, 0), (0, pad))).reshape(up_right.shape[0], -1))
        sums = doubling_sum(jnp.concatenate(pieces, 1), "dp", replicas)
        up_right = sums[:, :up_cols]
        emb_right = sums[:, up_cols : up_cols + emb_cols]
        if step == 0:
            norm_total = sums[:, up_cols + emb_cols :].reshape(1, -1)[:, :norm_len]
            norm_total = norm_total.reshape(norm_grads.shape[1:])

    up_approx = outer_t(up_left, up_right) / replicas
    emb_approx = outer_t(emb_left, emb_right) / replicas
    up_error_new = (up_field - up_approx)[None]
    emb_error_new = (emb_field - emb_approx)[None]
    up_moment_all_new = BETA * up_moment_all + up_approx
    emb_moment_all_new = BETA * emb_moment_all + emb_approx
    up_step = (up_approx + BETA * up_moment_all_new).astype(jnp.bfloat16)
    emb_step = (emb_approx + BETA * emb_moment_all_new).astype(jnp.bfloat16)
    up_count = up_moment.shape[0]
    emb_count = emb_moment.shape[0]
    up_moment_new = lax.dynamic_slice_in_dim(up_moment_all_new, dp_index * up_count, up_count, 0)
    emb_moment_new = lax.dynamic_slice_in_dim(
        emb_moment_all_new, dp_index * emb_count, emb_count, 0
    )
    norm_mean = norm_total / replicas
    norm_moment_new = BETA * norm_moment + norm_mean
    norm_step = norm_mean + BETA * norm_moment_new
    return (
        up_error_new,
        emb_error_new,
        up_moment_new,
        emb_moment_new,
        up_step,
        emb_step,
        norm_moment_new,
        norm_step,
    )


def solution(mesh):
    return jax.shard_map(
        per_device,
        mesh=mesh,
        in_specs=(
            P("dp", None),
            P("dp", "tensor"),
            P("dp"),
            P("dp", "tensor"),
            P("dp", None, "tensor"),
            P("dp", None, "tensor"),
            P("dp", "tensor"),
            P("dp", "tensor"),
            P("tensor", None),
            P("tensor", None),
            P(),
            P(),
            P("dp", None, None),
            P(),
        ),
        out_specs=(
            P("dp", None, "tensor"),
            P("dp", None, "tensor"),
            P("dp", "tensor"),
            P("dp", "tensor"),
            P(None, "tensor"),
            P(None, "tensor"),
            P(),
            P(),
        ),
        check_vma=False,
    )
```

```python
import math

import jax
import jax.numpy as jnp
from jax import lax
from jax.sharding import PartitionSpec as P

BETA = 0.9
HIGHEST = lax.Precision.HIGHEST
HIGH = lax.Precision.HIGH
ALL = ("dp", "tensor")


def log2_of(n):
    bits = n.bit_length() - 1
    assert 1 << bits == n
    return bits


def partner(bit, n):
    return [(i, i ^ (1 << bit)) for i in range(n)]


def doubling_sum(x, axes, n):
    for bit in range(log2_of(n)):
        x = x + lax.ppermute(x, axes, partner(bit, n))
    return x


def split_axis(shape):
    rows, lanes = shape
    if lanes % 256 == 0:
        return 1
    if rows % 16 == 0:
        return 0
    return 1 if lanes % 2 == 0 else 0


def halving_sum(x, axes, n, index, middle=None):
    plan = []
    for bit in range(log2_of(n)):
        axis = split_axis(x.shape)
        half = x.shape[axis] // 2
        low = lax.slice_in_dim(x, 0, half, axis=axis)
        high = lax.slice_in_dim(x, half, 2 * half, axis=axis)
        upper = ((index >> bit) & 1) == 1
        keep = jnp.where(upper, high, low)
        send = jnp.where(upper, low, high)
        x = keep + lax.ppermute(send, axes, partner(bit, n))
        plan.append((bit, axis, upper))
    if middle is not None:
        x = middle(x)
    for bit, axis, upper in reversed(plan):
        got = lax.ppermute(x, axes, partner(bit, n))
        x = jnp.where(
            upper, jnp.concatenate([got, x], axis), jnp.concatenate([x, got], axis)
        )
    return x


def scale_of(left_sum_t, rows):
    return lax.rsqrt(jnp.mean(left_sum_t * left_sum_t) + 1e-06) / math.sqrt(rows)


def normalized_t(left_sum_t, gram, rows):
    out = lax.dot_general(gram, left_sum_t, (((0,), (0,)), ((), ())), precision=HIGH)
    return out * scale_of(left_sum_t, rows)


def left_t(field, right_t):
    return lax.dot_general(right_t, field, (((1,), (1,)), ((), ())), precision=HIGH)


def right_t(field, left_t_):
    return lax.dot_general(left_t_, field, (((1,), (0,)), ((), ())), precision=HIGH)


def outer_t(left_t_, right_t_):
    return lax.dot_general(left_t_, right_t_, (((0,), (0,)), ((), ())), precision=HIGH)


def per_device(
    up_inputs,
    up_grad_out,
    emb_ids,
    emb_grad_out,
    up_error,
    emb_error,
    up_moment,
    emb_moment,
    up_start,
    emb_start,
    up_gram_inv,
    emb_gram_inv,
    norm_grads,
    norm_moment,
):
    replicas = lax.axis_size("dp")
    tensors = lax.axis_size("tensor")
    dp_index = lax.axis_index("dp")

    up_moment_all = lax.all_gather(up_moment, "dp", axis=0, tiled=True)
    emb_moment_all = lax.all_gather(emb_moment, "dp", axis=0, tiled=True)

    up_field = (
        lax.dot_general(
            up_inputs, up_grad_out, (((0,), (0,)), ((), ())), preferred_element_type=jnp.float32
        )
        + up_error[0]
    )
    vocab = emb_error.shape[1]
    one_hot_cols = (
        lax.broadcasted_iota(jnp.int32, (vocab, emb_ids.shape[0]), 0) == emb_ids[None, :]
    ).astype(jnp.bfloat16)
    emb_terms = lax.dot_general(
        one_hot_cols, emb_grad_out, (((1,), (0,)), ((), ())), preferred_element_type=jnp.float32
    )
    emb_field = emb_terms + emb_error[0]
    up_rows, up_cols = up_field.shape
    emb_rows, emb_cols = emb_field.shape

    norm_flat = norm_grads[0].reshape(1, -1)
    norm_len = norm_flat.shape[1]

    up_right = up_start.T
    emb_right = emb_start.T
    up_left = emb_left = None
    norm_total = None
    for step in range(up_gram_inv.shape[0]):
        parts = jnp.concatenate([left_t(up_field, up_right), left_t(emb_field, emb_right)], 1)
        sums = halving_sum(
            parts,
            "tensor",
            tensors,
            lax.axis_index("tensor"),
            lambda chunk: doubling_sum(chunk, "dp", replicas),
        )
        up_left = normalized_t(sums[:, :up_rows], up_gram_inv[step], up_rows)
        emb_left = normalized_t(sums[:, up_rows:], emb_gram_inv[step], emb_rows)
        pieces = [right_t(up_field, up_left), right_t(emb_field, emb_left)]
        if step == 0:
            pad = -norm_len % up_right.shape[0]
            pieces.append(jnp.pad(norm_flat, ((0, 0), (0, pad))).reshape(up_right.shape[0], -1))
        sums = doubling_sum(jnp.concatenate(pieces, 1), "dp", replicas)
        up_right = sums[:, :up_cols]
        emb_right = sums[:, up_cols : up_cols + emb_cols]
        if step == 0:
            norm_total = sums[:, up_cols + emb_cols :].reshape(1, -1)[:, :norm_len]
            norm_total = norm_total.reshape(norm_grads.shape[1:])

    up_approx = outer_t(up_left, up_right) / replicas
    emb_approx = outer_t(emb_left, emb_right) / replicas
    up_error_new = (up_field - up_approx)[None]
    emb_error_new = (emb_field - emb_approx)[None]
    up_step = (up_approx + BETA * (BETA * up_moment_all + up_approx)).astype(jnp.bfloat16)
    emb_step = (emb_approx + BETA * (BETA * emb_moment_all + emb_approx)).astype(jnp.bfloat16)
    up_count = up_moment.shape[0]
    emb_count = emb_moment.shape[0]
    up_local = lax.dynamic_slice_in_dim(up_left, dp_index * up_count, up_count, 1)
    emb_local = lax.dynamic_slice_in_dim(emb_left, dp_index * emb_count, emb_count, 1)
    up_moment_new = BETA * up_moment + outer_t(up_local, up_right) / replicas
    emb_moment_new = BETA * emb_moment + outer_t(emb_local, emb_right) / replicas
    norm_mean = norm_total / replicas
    norm_moment_new = BETA * norm_moment + norm_mean
    norm_step = norm_mean + BETA * norm_moment_new
    return (
        up_error_new,
        emb_error_new,
        up_moment_new,
        emb_moment_new,
        up_step,
        emb_step,
        norm_moment_new,
        norm_step,
    )


def solution(mesh):
    return jax.shard_map(
        per_device,
        mesh=mesh,
        in_specs=(
            P("dp", None),
            P("dp", "tensor"),
            P("dp"),
            P("dp", "tensor"),
            P("dp", None, "tensor"),
            P("dp", None, "tensor"),
            P("dp", "tensor"),
            P("dp", "tensor"),
            P("tensor", None),
            P("tensor", None),
            P(),
            P(),
            P("dp", None, None),
            P(),
        ),
        out_specs=(
            P("dp", None, "tensor"),
            P("dp", None, "tensor"),
            P("dp", "tensor"),
            P("dp", "tensor"),
            P(None, "tensor"),
            P(None, "tensor"),
            P(),
            P(),
        ),
        check_vma=False,
    )
```

```python
import math

import jax
import jax.numpy as jnp
from jax import lax
from jax.sharding import PartitionSpec as P

BETA = 0.9
HIGHEST = lax.Precision.HIGHEST
HIGH = lax.Precision.HIGH
ALL = ("dp", "tensor")


def log2_of(n):
    bits = n.bit_length() - 1
    assert 1 << bits == n
    return bits


def partner(bit, n):
    return [(i, i ^ (1 << bit)) for i in range(n)]


def doubling_sum(x, axes, n):
    for bit in range(log2_of(n)):
        x = x + lax.ppermute(x, axes, partner(bit, n))
    return x


def split_axis(shape):
    rows, lanes = shape
    if lanes % 256 == 0:
        return 1
    if rows % 16 == 0:
        return 0
    return 1 if lanes % 2 == 0 else 0


def halving_sum(x, axes, n, index, middle=None):
    plan = []
    for bit in range(log2_of(n)):
        axis = split_axis(x.shape)
        half = x.shape[axis] // 2
        low = lax.slice_in_dim(x, 0, half, axis=axis)
        high = lax.slice_in_dim(x, half, 2 * half, axis=axis)
        upper = ((index >> bit) & 1) == 1
        keep = jnp.where(upper, high, low)
        send = jnp.where(upper, low, high)
        x = keep + lax.ppermute(send, axes, partner(bit, n))
        plan.append((bit, axis, upper))
    if middle is not None:
        x = middle(x)
    for bit, axis, upper in reversed(plan):
        got = lax.ppermute(x, axes, partner(bit, n))
        x = jnp.where(
            upper, jnp.concatenate([got, x], axis), jnp.concatenate([x, got], axis)
        )
    return x


def scale_of(left_sum_t, rows):
    return lax.rsqrt(jnp.mean(left_sum_t * left_sum_t) + 1e-06) / math.sqrt(rows)


def normalized_t(left_sum_t, gram, rows):
    out = lax.dot_general(gram, left_sum_t, (((0,), (0,)), ((), ())), precision=HIGHEST)
    return out * scale_of(left_sum_t, rows)


def left_t(field, right_t):
    return lax.dot_general(right_t, field, (((1,), (1,)), ((), ())), precision=HIGH)


def right_t(field, left_t_):
    return lax.dot_general(left_t_, field, (((1,), (0,)), ((), ())), precision=HIGH)


def split_bf16(x):
    high = lax.reduce_precision(x, exponent_bits=8, mantissa_bits=7)
    return high.astype(jnp.bfloat16), (x - high).astype(jnp.bfloat16)


def outer_t(left_t_, right_t_):
    left_high, left_low = split_bf16(left_t_)
    right_high, right_low = split_bf16(right_t_)
    lhs = jnp.concatenate([left_high, left_high, left_low], 0)
    rhs = jnp.concatenate([right_high, right_low, right_high], 0)
    return lax.dot_general(
        lhs, rhs, (((0,), (0,)), ((), ())), preferred_element_type=jnp.float32
    )


def per_device(
    up_inputs,
    up_grad_out,
    emb_ids,
    emb_grad_out,
    up_error,
    emb_error,
    up_moment,
    emb_moment,
    up_start,
    emb_start,
    up_gram_inv,
    emb_gram_inv,
    norm_grads,
    norm_moment,
):
    replicas = lax.axis_size("dp")
    tensors = lax.axis_size("tensor")
    dp_index = lax.axis_index("dp")

    up_moment_all = lax.all_gather(up_moment, "dp", axis=0, tiled=True)
    emb_moment_all = lax.all_gather(emb_moment, "dp", axis=0, tiled=True)

    up_field = (
        lax.dot_general(
            up_inputs, up_grad_out, (((0,), (0,)), ((), ())), preferred_element_type=jnp.float32
        )
        + up_error[0]
    )
    vocab = emb_error.shape[1]
    one_hot_cols = (
        lax.broadcasted_iota(jnp.int32, (vocab, emb_ids.shape[0]), 0) == emb_ids[None, :]
    ).astype(jnp.bfloat16)
    emb_terms = lax.dot_general(
        one_hot_cols, emb_grad_out, (((1,), (0,)), ((), ())), preferred_element_type=jnp.float32
    )
    emb_field = emb_terms + emb_error[0]
    up_rows, up_cols = up_field.shape
    emb_rows, emb_cols = emb_field.shape

    norm_flat = norm_grads[0].reshape(1, -1)
    norm_len = norm_flat.shape[1]

    up_right = up_start.T
    emb_right = emb_start.T
    up_left = emb_left = None
    norm_total = None
    for step in range(up_gram_inv.shape[0]):
        parts = jnp.concatenate([left_t(up_field, up_right), left_t(emb_field, emb_right)], 1)
        sums = halving_sum(
            parts,
            "tensor",
            tensors,
            lax.axis_index("tensor"),
            lambda chunk: doubling_sum(chunk, "dp", replicas),
        )
        up_left = normalized_t(sums[:, :up_rows], up_gram_inv[step], up_rows)
        emb_left = normalized_t(sums[:, up_rows:], emb_gram_inv[step], emb_rows)
        pieces = [right_t(up_field, up_left), right_t(emb_field, emb_left)]
        if step == 0:
            pad = -norm_len % up_right.shape[0]
            pieces.append(jnp.pad(norm_flat, ((0, 0), (0, pad))).reshape(up_right.shape[0], -1))
        sums = doubling_sum(jnp.concatenate(pieces, 1), "dp", replicas)
        up_right = sums[:, :up_cols]
        emb_right = sums[:, up_cols : up_cols + emb_cols]
        if step == 0:
            norm_total = sums[:, up_cols + emb_cols :].reshape(1, -1)[:, :norm_len]
            norm_total = norm_total.reshape(norm_grads.shape[1:])

    up_approx = outer_t(up_left, up_right) / replicas
    emb_approx = outer_t(emb_left, emb_right) / replicas
    up_error_new = (up_field - up_approx)[None]
    emb_error_new = (emb_field - emb_approx)[None]
    up_moment_all_new = BETA * up_moment_all + up_approx
    emb_moment_all_new = BETA * emb_moment_all + emb_approx
    up_step = (up_approx + BETA * up_moment_all_new).astype(jnp.bfloat16)
    emb_step = (emb_approx + BETA * emb_moment_all_new).astype(jnp.bfloat16)
    up_count = up_moment.shape[0]
    emb_count = emb_moment.shape[0]
    up_moment_new = lax.dynamic_slice_in_dim(up_moment_all_new, dp_index * up_count, up_count, 0)
    emb_moment_new = lax.dynamic_slice_in_dim(
        emb_moment_all_new, dp_index * emb_count, emb_count, 0
    )
    norm_mean = norm_total / replicas
    norm_moment_new = BETA * norm_moment + norm_mean
    norm_step = norm_mean + BETA * norm_moment_new
    return (
        up_error_new,
        emb_error_new,
        up_moment_new,
        emb_moment_new,
        up_step,
        emb_step,
        norm_moment_new,
        norm_step,
    )


def solution(mesh):
    return jax.shard_map(
        per_device,
        mesh=mesh,
        in_specs=(
            P("dp", None),
            P("dp", "tensor"),
            P("dp"),
            P("dp", "tensor"),
            P("dp", None, "tensor"),
            P("dp", None, "tensor"),
            P("dp", "tensor"),
            P("dp", "tensor"),
            P("tensor", None),
            P("tensor", None),
            P(),
            P(),
            P("dp", None, None),
            P(),
        ),
        out_specs=(
            P("dp", None, "tensor"),
            P("dp", None, "tensor"),
            P("dp", "tensor"),
            P("dp", "tensor"),
            P(None, "tensor"),
            P(None, "tensor"),
            P(),
            P(),
        ),
        check_vma=False,
    )
```

```python
import math

import jax
import jax.numpy as jnp
from jax import lax
from jax.sharding import PartitionSpec as P

BETA = 0.9
HIGHEST = lax.Precision.HIGHEST
HIGH = lax.Precision.HIGH
ALL = ("dp", "tensor")


def log2_of(n):
    bits = n.bit_length() - 1
    assert 1 << bits == n
    return bits


def partner(bit, n):
    return [(i, i ^ (1 << bit)) for i in range(n)]


def doubling_sum(x, axes, n):
    for bit in range(log2_of(n)):
        x = x + lax.ppermute(x, axes, partner(bit, n))
    return x


def split_axis(shape):
    rows, lanes = shape
    if lanes % 256 == 0:
        return 1
    if rows % 16 == 0:
        return 0
    return 1 if lanes % 2 == 0 else 0


def halving_sum(x, axes, n, index, middle=None):
    plan = []
    for bit in range(log2_of(n)):
        axis = split_axis(x.shape)
        half = x.shape[axis] // 2
        low = lax.slice_in_dim(x, 0, half, axis=axis)
        high = lax.slice_in_dim(x, half, 2 * half, axis=axis)
        upper = ((index >> bit) & 1) == 1
        keep = jnp.where(upper, high, low)
        send = jnp.where(upper, low, high)
        x = keep + lax.ppermute(send, axes, partner(bit, n))
        plan.append((bit, axis, upper))
    if middle is not None:
        x = middle(x)
    for bit, axis, upper in reversed(plan):
        got = lax.ppermute(x, axes, partner(bit, n))
        x = jnp.where(
            upper, jnp.concatenate([got, x], axis), jnp.concatenate([x, got], axis)
        )
    return x


def scale_of(left_sum_t, rows):
    return lax.rsqrt(jnp.mean(left_sum_t * left_sum_t) + 1e-06) / math.sqrt(rows)


def normalized_t(left_sum_t, gram, rows):
    return outer_t(gram, left_sum_t) * scale_of(left_sum_t, rows)


def left_t(field, right_t):
    return lax.dot_general(right_t, field, (((1,), (1,)), ((), ())), precision=HIGH)


def right_t(field, left_t_):
    return lax.dot_general(left_t_, field, (((1,), (0,)), ((), ())), precision=HIGH)


def split_bf16(x):
    high = lax.reduce_precision(x, exponent_bits=8, mantissa_bits=7)
    return high.astype(jnp.bfloat16), (x - high).astype(jnp.bfloat16)


def outer_t(left_t_, right_t_):
    left_high, left_low = split_bf16(left_t_)
    right_high, right_low = split_bf16(right_t_)
    lhs = jnp.concatenate([left_high, left_high, left_low], 0)
    rhs = jnp.concatenate([right_high, right_low, right_high], 0)
    return lax.dot_general(
        lhs, rhs, (((0,), (0,)), ((), ())), preferred_element_type=jnp.float32
    )


def per_device(
    up_inputs,
    up_grad_out,
    emb_ids,
    emb_grad_out,
    up_error,
    emb_error,
    up_moment,
    emb_moment,
    up_start,
    emb_start,
    up_gram_inv,
    emb_gram_inv,
    norm_grads,
    norm_moment,
):
    replicas = lax.axis_size("dp")
    tensors = lax.axis_size("tensor")
    dp_index = lax.axis_index("dp")

    up_moment_all = lax.all_gather(up_moment, "dp", axis=0, tiled=True)
    emb_moment_all = lax.all_gather(emb_moment, "dp", axis=0, tiled=True)

    up_field = (
        lax.dot_general(
            up_inputs, up_grad_out, (((0,), (0,)), ((), ())), preferred_element_type=jnp.float32
        )
        + up_error[0]
    )
    vocab = emb_error.shape[1]
    one_hot_cols = (
        lax.broadcasted_iota(jnp.int32, (vocab, emb_ids.shape[0]), 0) == emb_ids[None, :]
    ).astype(jnp.bfloat16)
    emb_terms = lax.dot_general(
        one_hot_cols, emb_grad_out, (((1,), (0,)), ((), ())), preferred_element_type=jnp.float32
    )
    emb_field = emb_terms + emb_error[0]
    up_rows, up_cols = up_field.shape
    emb_rows, emb_cols = emb_field.shape

    norm_flat = norm_grads[0].reshape(1, -1)
    norm_len = norm_flat.shape[1]

    up_right = up_start.T
    emb_right = emb_start.T
    up_left = emb_left = None
    norm_total = None
    for step in range(up_gram_inv.shape[0]):
        parts = jnp.concatenate([left_t(up_field, up_right), left_t(emb_field, emb_right)], 1)
        sums = halving_sum(
            parts,
            "tensor",
            tensors,
            lax.axis_index("tensor"),
            lambda chunk: doubling_sum(chunk, "dp", replicas),
        )
        up_left = normalized_t(sums[:, :up_rows], up_gram_inv[step], up_rows)
        emb_left = normalized_t(sums[:, up_rows:], emb_gram_inv[step], emb_rows)
        pieces = [right_t(up_field, up_left), right_t(emb_field, emb_left)]
        if step == 0:
            pad = -norm_len % up_right.shape[0]
            pieces.append(jnp.pad(norm_flat, ((0, 0), (0, pad))).reshape(up_right.shape[0], -1))
        sums = doubling_sum(jnp.concatenate(pieces, 1), "dp", replicas)
        up_right = sums[:, :up_cols]
        emb_right = sums[:, up_cols : up_cols + emb_cols]
        if step == 0:
            norm_total = sums[:, up_cols + emb_cols :].reshape(1, -1)[:, :norm_len]
            norm_total = norm_total.reshape(norm_grads.shape[1:])

    up_approx = outer_t(up_left, up_right) / replicas
    emb_approx = outer_t(emb_left, emb_right) / replicas
    up_error_new = (up_field - up_approx)[None]
    emb_error_new = (emb_field - emb_approx)[None]
    up_moment_all_new = BETA * up_moment_all + up_approx
    emb_moment_all_new = BETA * emb_moment_all + emb_approx
    up_step = (up_approx + BETA * up_moment_all_new).astype(jnp.bfloat16)
    emb_step = (emb_approx + BETA * emb_moment_all_new).astype(jnp.bfloat16)
    up_count = up_moment.shape[0]
    emb_count = emb_moment.shape[0]
    up_moment_new = lax.dynamic_slice_in_dim(up_moment_all_new, dp_index * up_count, up_count, 0)
    emb_moment_new = lax.dynamic_slice_in_dim(
        emb_moment_all_new, dp_index * emb_count, emb_count, 0
    )
    norm_mean = norm_total / replicas
    norm_moment_new = BETA * norm_moment + norm_mean
    norm_step = norm_mean + BETA * norm_moment_new
    return (
        up_error_new,
        emb_error_new,
        up_moment_new,
        emb_moment_new,
        up_step,
        emb_step,
        norm_moment_new,
        norm_step,
    )


def solution(mesh):
    return jax.shard_map(
        per_device,
        mesh=mesh,
        in_specs=(
            P("dp", None),
            P("dp", "tensor"),
            P("dp"),
            P("dp", "tensor"),
            P("dp", None, "tensor"),
            P("dp", None, "tensor"),
            P("dp", "tensor"),
            P("dp", "tensor"),
            P("tensor", None),
            P("tensor", None),
            P(),
            P(),
            P("dp", None, None),
            P(),
        ),
        out_specs=(
            P("dp", None, "tensor"),
            P("dp", None, "tensor"),
            P("dp", "tensor"),
            P("dp", "tensor"),
            P(None, "tensor"),
            P(None, "tensor"),
            P(),
            P(),
        ),
        check_vma=False,
    )
```

```python
import math

import jax
import jax.numpy as jnp
from jax import lax
from jax.sharding import PartitionSpec as P

BETA = 0.9
HIGHEST = lax.Precision.HIGHEST
HIGH = lax.Precision.HIGH
ALL = ("dp", "tensor")


def log2_of(n):
    bits = n.bit_length() - 1
    assert 1 << bits == n
    return bits


def partner(bit, n):
    return [(i, i ^ (1 << bit)) for i in range(n)]


def doubling_sum(x, axes, n):
    for bit in range(log2_of(n)):
        x = x + lax.ppermute(x, axes, partner(bit, n))
    return x


def split_axis(shape):
    rows, lanes = shape
    if lanes % 256 == 0:
        return 1
    if rows % 16 == 0:
        return 0
    return 1 if lanes % 2 == 0 else 0


def halving_sum(x, axes, n, index, middle=None):
    plan = []
    for bit in range(log2_of(n)):
        axis = split_axis(x.shape)
        half = x.shape[axis] // 2
        low = lax.slice_in_dim(x, 0, half, axis=axis)
        high = lax.slice_in_dim(x, half, 2 * half, axis=axis)
        upper = ((index >> bit) & 1) == 1
        keep = jnp.where(upper, high, low)
        send = jnp.where(upper, low, high)
        x = keep + lax.ppermute(send, axes, partner(bit, n))
        plan.append((bit, axis, upper))
    if middle is not None:
        x = middle(x)
    for bit, axis, upper in reversed(plan):
        got = lax.ppermute(x, axes, partner(bit, n))
        x = jnp.where(
            upper, jnp.concatenate([got, x], axis), jnp.concatenate([x, got], axis)
        )
    return x


def scale_of(left_sum_t, rows):
    return lax.rsqrt(jnp.mean(left_sum_t * left_sum_t) + 1e-06) / math.sqrt(rows)


def normalized_t(left_sum_t, gram, rows):
    out = lax.dot_general(gram, left_sum_t, (((0,), (0,)), ((), ())), precision=HIGHEST)
    return out * scale_of(left_sum_t, rows)


def left_t(field, right_t):
    return lax.dot_general(right_t, field, (((1,), (1,)), ((), ())), precision=HIGH)


def right_t(field, left_t_):
    return lax.dot_general(left_t_, field, (((1,), (0,)), ((), ())), precision=HIGH)


def outer_t(left_t_, right_t_):
    return lax.dot_general(left_t_, right_t_, (((0,), (0,)), ((), ())), precision=HIGH)


def per_device(
    up_inputs,
    up_grad_out,
    emb_ids,
    emb_grad_out,
    up_error,
    emb_error,
    up_moment,
    emb_moment,
    up_start,
    emb_start,
    up_gram_inv,
    emb_gram_inv,
    norm_grads,
    norm_moment,
):
    replicas = lax.axis_size("dp")
    tensors = lax.axis_size("tensor")
    dp_index = lax.axis_index("dp")

    up_moment_all = lax.all_gather(up_moment, "dp", axis=0, tiled=True)
    emb_moment_all = lax.all_gather(emb_moment, "dp", axis=0, tiled=True)

    up_field = (
        lax.dot_general(
            up_inputs, up_grad_out, (((0,), (0,)), ((), ())), preferred_element_type=jnp.float32
        )
        + up_error[0]
    )
    vocab = emb_error.shape[1]
    one_hot_cols = (
        lax.broadcasted_iota(jnp.int32, (vocab, emb_ids.shape[0]), 0) == emb_ids[None, :]
    ).astype(jnp.bfloat16)
    emb_terms = lax.dot_general(
        one_hot_cols, emb_grad_out, (((1,), (0,)), ((), ())), preferred_element_type=jnp.float32
    )
    emb_field = emb_terms + emb_error[0]
    up_rows, up_cols = up_field.shape
    emb_rows, emb_cols = emb_field.shape

    norm_flat = norm_grads[0].reshape(1, -1)
    norm_len = norm_flat.shape[1]

    up_right = up_start.T
    emb_right = emb_start.T
    up_left = emb_left = None
    norm_total = None
    for step in range(up_gram_inv.shape[0]):
        parts = jnp.concatenate([left_t(up_field, up_right), left_t(emb_field, emb_right)], 1)
        sums = halving_sum(parts, ALL, replicas * tensors, dp_index * tensors + lax.axis_index("tensor"))
        up_left = normalized_t(sums[:, :up_rows], up_gram_inv[step], up_rows)
        emb_left = normalized_t(sums[:, up_rows:], emb_gram_inv[step], emb_rows)
        pieces = [right_t(up_field, up_left), right_t(emb_field, emb_left)]
        if step == 0:
            pad = -norm_len % up_right.shape[0]
            pieces.append(jnp.pad(norm_flat, ((0, 0), (0, pad))).reshape(up_right.shape[0], -1))
        sums = doubling_sum(jnp.concatenate(pieces, 1), "dp", replicas)
        up_right = sums[:, :up_cols]
        emb_right = sums[:, up_cols : up_cols + emb_cols]
        if step == 0:
            norm_total = sums[:, up_cols + emb_cols :].reshape(1, -1)[:, :norm_len]
            norm_total = norm_total.reshape(norm_grads.shape[1:])

    up_approx = outer_t(up_left, up_right) / replicas
    emb_approx = outer_t(emb_left, emb_right) / replicas
    up_error_new = (up_field - up_approx)[None]
    emb_error_new = (emb_field - emb_approx)[None]
    up_moment_all_new = BETA * up_moment_all + up_approx
    emb_moment_all_new = BETA * emb_moment_all + emb_approx
    up_step = (up_approx + BETA * up_moment_all_new).astype(jnp.bfloat16)
    emb_step = (emb_approx + BETA * emb_moment_all_new).astype(jnp.bfloat16)
    up_count = up_moment.shape[0]
    emb_count = emb_moment.shape[0]
    up_moment_new = lax.dynamic_slice_in_dim(up_moment_all_new, dp_index * up_count, up_count, 0)
    emb_moment_new = lax.dynamic_slice_in_dim(
        emb_moment_all_new, dp_index * emb_count, emb_count, 0
    )
    norm_mean = norm_total / replicas
    norm_moment_new = BETA * norm_moment + norm_mean
    norm_step = norm_mean + BETA * norm_moment_new
    return (
        up_error_new,
        emb_error_new,
        up_moment_new,
        emb_moment_new,
        up_step,
        emb_step,
        norm_moment_new,
        norm_step,
    )


def solution(mesh):
    return jax.shard_map(
        per_device,
        mesh=mesh,
        in_specs=(
            P("dp", None),
            P("dp", "tensor"),
            P("dp"),
            P("dp", "tensor"),
            P("dp", None, "tensor"),
            P("dp", None, "tensor"),
            P("dp", "tensor"),
            P("dp", "tensor"),
            P("tensor", None),
            P("tensor", None),
            P(),
            P(),
            P("dp", None, None),
            P(),
        ),
        out_specs=(
            P("dp", None, "tensor"),
            P("dp", None, "tensor"),
            P("dp", "tensor"),
            P("dp", "tensor"),
            P(None, "tensor"),
            P(None, "tensor"),
            P(),
            P(),
        ),
        check_vma=False,
    )
```

```python
import math

import jax
import jax.numpy as jnp
from jax import lax
from jax.sharding import PartitionSpec as P

BETA = 0.9
HIGHEST = lax.Precision.HIGHEST
HIGH = lax.Precision.HIGH
ALL = ("dp", "tensor")


def log2_of(n):
    bits = n.bit_length() - 1
    assert 1 << bits == n
    return bits


def partner(bit, n):
    return [(i, i ^ (1 << bit)) for i in range(n)]


def doubling_sum(x, axes, n):
    for bit in range(log2_of(n)):
        x = x + lax.ppermute(x, axes, partner(bit, n))
    return x


def split_axis(shape):
    rows, lanes = shape
    if lanes % 256 == 0:
        return 1
    if rows % 16 == 0:
        return 0
    return 1 if lanes % 2 == 0 else 0


def halving_sum(x, axes, n, index, middle=None):
    plan = []
    for bit in range(log2_of(n)):
        axis = split_axis(x.shape)
        half = x.shape[axis] // 2
        low = lax.slice_in_dim(x, 0, half, axis=axis)
        high = lax.slice_in_dim(x, half, 2 * half, axis=axis)
        upper = ((index >> bit) & 1) == 1
        keep = jnp.where(upper, high, low)
        send = jnp.where(upper, low, high)
        x = keep + lax.ppermute(send, axes, partner(bit, n))
        plan.append((bit, axis, upper))
    if middle is not None:
        x = middle(x)
    for bit, axis, upper in reversed(plan):
        got = lax.ppermute(x, axes, partner(bit, n))
        x = jnp.where(
            upper, jnp.concatenate([got, x], axis), jnp.concatenate([x, got], axis)
        )
    return x


def scale_of(left_sum_t, rows):
    return lax.rsqrt(jnp.mean(left_sum_t * left_sum_t) + 1e-06) / math.sqrt(rows)


def normalized_t(left_sum_t, gram, rows):
    out = lax.dot_general(gram, left_sum_t, (((0,), (0,)), ((), ())), precision=HIGHEST)
    return out * scale_of(left_sum_t, rows)


def left_t(field, right_t):
    return lax.dot_general(right_t, field, (((1,), (1,)), ((), ())), precision=HIGH)


def right_t(field, left_t_):
    return lax.dot_general(left_t_, field, (((1,), (0,)), ((), ())), precision=HIGH)


def split_bf16(x):
    high = lax.reduce_precision(x, exponent_bits=8, mantissa_bits=7)
    return high.astype(jnp.bfloat16), (x - high).astype(jnp.bfloat16)


def outer_t(left_t_, right_t_):
    left_high, left_low = split_bf16(left_t_)
    right_high, right_low = split_bf16(right_t_)
    lhs = jnp.concatenate([left_high, left_high, left_low], 0)
    rhs = jnp.concatenate([right_high, right_low, right_high], 0)
    return lax.dot_general(
        lhs, rhs, (((0,), (0,)), ((), ())), preferred_element_type=jnp.float32
    )


def per_device(
    up_inputs,
    up_grad_out,
    emb_ids,
    emb_grad_out,
    up_error,
    emb_error,
    up_moment,
    emb_moment,
    up_start,
    emb_start,
    up_gram_inv,
    emb_gram_inv,
    norm_grads,
    norm_moment,
):
    replicas = lax.axis_size("dp")
    tensors = lax.axis_size("tensor")
    dp_index = lax.axis_index("dp")

    up_moment_all = lax.all_gather(up_moment, "dp", axis=0, tiled=True)
    emb_moment_all = lax.all_gather(emb_moment, "dp", axis=0, tiled=True)

    up_field = (
        lax.dot_general(
            up_inputs, up_grad_out, (((0,), (0,)), ((), ())), preferred_element_type=jnp.float32
        )
        + up_error[0]
    )
    vocab = emb_error.shape[1]
    one_hot_cols = (
        lax.broadcasted_iota(jnp.int32, (vocab, emb_ids.shape[0]), 0) == emb_ids[None, :]
    ).astype(jnp.bfloat16)
    emb_terms = lax.dot_general(
        one_hot_cols, emb_grad_out, (((1,), (0,)), ((), ())), preferred_element_type=jnp.float32
    )
    emb_field = emb_terms + emb_error[0]
    up_rows, up_cols = up_field.shape
    emb_rows, emb_cols = emb_field.shape

    norm_flat = norm_grads[0].reshape(1, -1)
    norm_len = norm_flat.shape[1]

    up_right = up_start.T
    emb_right = emb_start.T
    up_left = emb_left = None
    norm_total = None
    for step in range(up_gram_inv.shape[0]):
        parts = jnp.concatenate([left_t(up_field, up_right), left_t(emb_field, emb_right)], 1)
        sums = halving_sum(parts, ALL, replicas * tensors, dp_index * tensors + lax.axis_index("tensor"))
        up_left = normalized_t(sums[:, :up_rows], up_gram_inv[step], up_rows)
        emb_left = normalized_t(sums[:, up_rows:], emb_gram_inv[step], emb_rows)
        pieces = [right_t(up_field, up_left), right_t(emb_field, emb_left)]
        if step == 0:
            pad = -norm_len % up_right.shape[0]
            pieces.append(jnp.pad(norm_flat, ((0, 0), (0, pad))).reshape(up_right.shape[0], -1))
        sums = doubling_sum(jnp.concatenate(pieces, 1), "dp", replicas)
        up_right = sums[:, :up_cols]
        emb_right = sums[:, up_cols : up_cols + emb_cols]
        if step == 0:
            norm_total = sums[:, up_cols + emb_cols :].reshape(1, -1)[:, :norm_len]
            norm_total = norm_total.reshape(norm_grads.shape[1:])

    up_approx = outer_t(up_left, up_right) / replicas
    emb_approx = outer_t(emb_left, emb_right) / replicas
    up_error_new = (up_field - up_approx)[None]
    emb_error_new = (emb_field - emb_approx)[None]
    up_moment_all_new = BETA * up_moment_all + up_approx
    emb_moment_all_new = BETA * emb_moment_all + emb_approx
    up_step = (up_approx + BETA * up_moment_all_new).astype(jnp.bfloat16)
    emb_step = (emb_approx + BETA * emb_moment_all_new).astype(jnp.bfloat16)
    up_count = up_moment.shape[0]
    emb_count = emb_moment.shape[0]
    up_moment_new = lax.dynamic_slice_in_dim(up_moment_all_new, dp_index * up_count, up_count, 0)
    emb_moment_new = lax.dynamic_slice_in_dim(
        emb_moment_all_new, dp_index * emb_count, emb_count, 0
    )
    norm_mean = norm_total / replicas
    norm_moment_new = BETA * norm_moment + norm_mean
    norm_step = norm_mean + BETA * norm_moment_new
    return (
        up_error_new,
        emb_error_new,
        up_moment_new,
        emb_moment_new,
        up_step,
        emb_step,
        norm_moment_new,
        norm_step,
    )


def solution(mesh):
    return jax.shard_map(
        per_device,
        mesh=mesh,
        in_specs=(
            P("dp", None),
            P("dp", "tensor"),
            P("dp"),
            P("dp", "tensor"),
            P("dp", None, "tensor"),
            P("dp", None, "tensor"),
            P("dp", "tensor"),
            P("dp", "tensor"),
            P("tensor", None),
            P("tensor", None),
            P(),
            P(),
            P("dp", None, None),
            P(),
        ),
        out_specs=(
            P("dp", None, "tensor"),
            P("dp", None, "tensor"),
            P("dp", "tensor"),
            P("dp", "tensor"),
            P(None, "tensor"),
            P(None, "tensor"),
            P(),
            P(),
        ),
        check_vma=False,
    )
```

```python
import math

import jax
import jax.numpy as jnp
from jax import lax
from jax.sharding import PartitionSpec as P

BETA = 0.9
HIGHEST = lax.Precision.HIGHEST
HIGH = lax.Precision.HIGH
ALL = ("dp", "tensor")


def log2_of(n):
    bits = n.bit_length() - 1
    assert 1 << bits == n
    return bits


def partner(bit, n):
    return [(i, i ^ (1 << bit)) for i in range(n)]


def doubling_sum(x, axes, n):
    for bit in range(log2_of(n)):
        x = x + lax.ppermute(x, axes, partner(bit, n))
    return x


def split_axis(shape):
    rows, lanes = shape
    if lanes % 256 == 0:
        return 1
    if rows % 16 == 0:
        return 0
    return 1 if lanes % 2 == 0 else 0


def halving_sum(x, axes, n, index, middle=None):
    plan = []
    for bit in range(log2_of(n)):
        axis = split_axis(x.shape)
        half = x.shape[axis] // 2
        low = lax.slice_in_dim(x, 0, half, axis=axis)
        high = lax.slice_in_dim(x, half, 2 * half, axis=axis)
        upper = ((index >> bit) & 1) == 1
        keep = jnp.where(upper, high, low)
        send = jnp.where(upper, low, high)
        x = keep + lax.ppermute(send, axes, partner(bit, n))
        plan.append((bit, axis, upper))
    if middle is not None:
        x = middle(x)
    for bit, axis, upper in reversed(plan):
        got = lax.ppermute(x, axes, partner(bit, n))
        x = jnp.where(
            upper, jnp.concatenate([got, x], axis), jnp.concatenate([x, got], axis)
        )
    return x


def scale_of(left_sum_t, rows):
    return lax.rsqrt(jnp.mean(left_sum_t * left_sum_t) + 1e-06) / math.sqrt(rows)


def normalized_t(left_sum_t, gram, rows):
    out = lax.dot_general(gram, left_sum_t, (((0,), (0,)), ((), ())), precision=HIGHEST)
    return out * scale_of(left_sum_t, rows)


def left_t(field, right_t):
    return lax.dot_general(right_t, field, (((1,), (1,)), ((), ())), precision=HIGH)


def right_t(field, left_t_):
    return lax.dot_general(left_t_, field, (((1,), (0,)), ((), ())), precision=HIGH)


def split_bf16(x):
    high = lax.reduce_precision(x, exponent_bits=8, mantissa_bits=7)
    return high.astype(jnp.bfloat16), (x - high).astype(jnp.bfloat16)


def outer_t(left_t_, right_t_):
    left_high, left_low = split_bf16(left_t_)
    right_high, right_low = split_bf16(right_t_)
    lhs = jnp.concatenate([left_high, left_high, left_low], 0)
    rhs = jnp.concatenate([right_high, right_low, right_high], 0)
    return lax.dot_general(
        lhs, rhs, (((0,), (0,)), ((), ())), preferred_element_type=jnp.float32
    )


def per_device(
    up_inputs,
    up_grad_out,
    emb_ids,
    emb_grad_out,
    up_error,
    emb_error,
    up_moment,
    emb_moment,
    up_start,
    emb_start,
    up_gram_inv,
    emb_gram_inv,
    norm_grads,
    norm_moment,
):
    replicas = lax.axis_size("dp")
    tensors = lax.axis_size("tensor")
    dp_index = lax.axis_index("dp")

    up_moment_all = lax.all_gather(up_moment, "dp", axis=0, tiled=True)
    emb_moment_all = lax.all_gather(emb_moment, "dp", axis=0, tiled=True)

    up_field = (
        lax.dot_general(
            up_inputs, up_grad_out, (((0,), (0,)), ((), ())), preferred_element_type=jnp.float32
        )
        + up_error[0]
    )
    vocab = emb_error.shape[1]
    one_hot_cols = (
        lax.broadcasted_iota(jnp.int32, (vocab, emb_ids.shape[0]), 0) == emb_ids[None, :]
    ).astype(jnp.bfloat16)
    emb_terms = lax.dot_general(
        one_hot_cols, emb_grad_out, (((1,), (0,)), ((), ())), preferred_element_type=jnp.float32
    )
    emb_field = emb_terms + emb_error[0]
    up_rows, up_cols = up_field.shape
    emb_rows, emb_cols = emb_field.shape

    norm_flat = norm_grads[0].reshape(1, -1)
    norm_len = norm_flat.shape[1]

    up_right = up_start.T
    emb_right = emb_start.T
    up_left = emb_left = None
    norm_total = None
    for step in range(up_gram_inv.shape[0]):
        parts = jnp.concatenate([left_t(up_field, up_right), left_t(emb_field, emb_right)], 1)
        sums = halving_sum(parts, ALL, replicas * tensors, dp_index * tensors + lax.axis_index("tensor"))
        up_left = normalized_t(sums[:, :up_rows], up_gram_inv[step], up_rows)
        emb_left = normalized_t(sums[:, up_rows:], emb_gram_inv[step], emb_rows)
        pieces = [right_t(up_field, up_left), right_t(emb_field, emb_left)]
        if step == 0:
            pad = -norm_len % up_right.shape[0]
            pieces.append(jnp.pad(norm_flat, ((0, 0), (0, pad))).reshape(up_right.shape[0], -1))
        joined = jnp.concatenate(pieces, 1)
        width = 128 * replicas
        joined = jnp.pad(joined, ((0, 0), (0, -joined.shape[1] % width)))
        sums = halving_sum(joined, "dp", replicas, dp_index)
        up_right = sums[:, :up_cols]
        emb_right = sums[:, up_cols : up_cols + emb_cols]
        if step == 0:
            norm_total = sums[:, up_cols + emb_cols :].reshape(1, -1)[:, :norm_len]
            norm_total = norm_total.reshape(norm_grads.shape[1:])

    up_approx = outer_t(up_left, up_right) / replicas
    emb_approx = outer_t(emb_left, emb_right) / replicas
    up_error_new = (up_field - up_approx)[None]
    emb_error_new = (emb_field - emb_approx)[None]
    up_moment_all_new = BETA * up_moment_all + up_approx
    emb_moment_all_new = BETA * emb_moment_all + emb_approx
    up_step = (up_approx + BETA * up_moment_all_new).astype(jnp.bfloat16)
    emb_step = (emb_approx + BETA * emb_moment_all_new).astype(jnp.bfloat16)
    up_count = up_moment.shape[0]
    emb_count = emb_moment.shape[0]
    up_moment_new = lax.dynamic_slice_in_dim(up_moment_all_new, dp_index * up_count, up_count, 0)
    emb_moment_new = lax.dynamic_slice_in_dim(
        emb_moment_all_new, dp_index * emb_count, emb_count, 0
    )
    norm_mean = norm_total / replicas
    norm_moment_new = BETA * norm_moment + norm_mean
    norm_step = norm_mean + BETA * norm_moment_new
    return (
        up_error_new,
        emb_error_new,
        up_moment_new,
        emb_moment_new,
        up_step,
        emb_step,
        norm_moment_new,
        norm_step,
    )


def solution(mesh):
    return jax.shard_map(
        per_device,
        mesh=mesh,
        in_specs=(
            P("dp", None),
            P("dp", "tensor"),
            P("dp"),
            P("dp", "tensor"),
            P("dp", None, "tensor"),
            P("dp", None, "tensor"),
            P("dp", "tensor"),
            P("dp", "tensor"),
            P("tensor", None),
            P("tensor", None),
            P(),
            P(),
            P("dp", None, None),
            P(),
        ),
        out_specs=(
            P("dp", None, "tensor"),
            P("dp", None, "tensor"),
            P("dp", "tensor"),
            P("dp", "tensor"),
            P(None, "tensor"),
            P(None, "tensor"),
            P(),
            P(),
        ),
        check_vma=False,
    )
```

```python
import math

import jax
import jax.numpy as jnp
from jax import lax
from jax.sharding import PartitionSpec as P

BETA = 0.9
HIGHEST = lax.Precision.HIGHEST
HIGH = lax.Precision.HIGH
ALL = ("dp", "tensor")


def log2_of(n):
    bits = n.bit_length() - 1
    assert 1 << bits == n
    return bits


def partner(bit, n):
    return [(i, i ^ (1 << bit)) for i in range(n)]


def doubling_sum(x, axes, n):
    for bit in reversed(range(log2_of(n))):
        x = x + lax.ppermute(x, axes, partner(bit, n))
    return x


def split_axis(shape):
    rows, lanes = shape
    if lanes % 256 == 0:
        return 1
    if rows % 16 == 0:
        return 0
    return 1 if lanes % 2 == 0 else 0


def halving_sum(x, axes, n, index, middle=None):
    plan = []
    for bit in range(log2_of(n)):
        axis = split_axis(x.shape)
        half = x.shape[axis] // 2
        low = lax.slice_in_dim(x, 0, half, axis=axis)
        high = lax.slice_in_dim(x, half, 2 * half, axis=axis)
        upper = ((index >> bit) & 1) == 1
        keep = jnp.where(upper, high, low)
        send = jnp.where(upper, low, high)
        x = keep + lax.ppermute(send, axes, partner(bit, n))
        plan.append((bit, axis, upper))
    if middle is not None:
        x = middle(x)
    for bit, axis, upper in reversed(plan):
        got = lax.ppermute(x, axes, partner(bit, n))
        x = jnp.where(
            upper, jnp.concatenate([got, x], axis), jnp.concatenate([x, got], axis)
        )
    return x


def scale_of(left_sum_t, rows):
    return lax.rsqrt(jnp.mean(left_sum_t * left_sum_t) + 1e-06) / math.sqrt(rows)


def normalized_t(left_sum_t, gram, rows):
    out = lax.dot_general(gram, left_sum_t, (((0,), (0,)), ((), ())), precision=HIGHEST)
    return out * scale_of(left_sum_t, rows)


def left_t(field, right_t):
    return lax.dot_general(right_t, field, (((1,), (1,)), ((), ())), precision=HIGH)


def right_t(field, left_t_):
    return lax.dot_general(left_t_, field, (((1,), (0,)), ((), ())), precision=HIGH)


def split_bf16(x):
    high = lax.reduce_precision(x, exponent_bits=8, mantissa_bits=7)
    return high.astype(jnp.bfloat16), (x - high).astype(jnp.bfloat16)


def outer_t(left_t_, right_t_):
    left_high, left_low = split_bf16(left_t_)
    right_high, right_low = split_bf16(right_t_)
    lhs = jnp.concatenate([left_high, left_high, left_low], 0)
    rhs = jnp.concatenate([right_high, right_low, right_high], 0)
    return lax.dot_general(
        lhs, rhs, (((0,), (0,)), ((), ())), preferred_element_type=jnp.float32
    )


def per_device(
    up_inputs,
    up_grad_out,
    emb_ids,
    emb_grad_out,
    up_error,
    emb_error,
    up_moment,
    emb_moment,
    up_start,
    emb_start,
    up_gram_inv,
    emb_gram_inv,
    norm_grads,
    norm_moment,
):
    replicas = lax.axis_size("dp")
    tensors = lax.axis_size("tensor")
    dp_index = lax.axis_index("dp")

    up_moment_all = lax.all_gather(up_moment, "dp", axis=0, tiled=True)
    emb_moment_all = lax.all_gather(emb_moment, "dp", axis=0, tiled=True)

    up_field = (
        lax.dot_general(
            up_inputs, up_grad_out, (((0,), (0,)), ((), ())), preferred_element_type=jnp.float32
        )
        + up_error[0]
    )
    vocab = emb_error.shape[1]
    one_hot_cols = (
        lax.broadcasted_iota(jnp.int32, (vocab, emb_ids.shape[0]), 0) == emb_ids[None, :]
    ).astype(jnp.bfloat16)
    emb_terms = lax.dot_general(
        one_hot_cols, emb_grad_out, (((1,), (0,)), ((), ())), preferred_element_type=jnp.float32
    )
    emb_field = emb_terms + emb_error[0]
    up_rows, up_cols = up_field.shape
    emb_rows, emb_cols = emb_field.shape

    norm_flat = norm_grads[0].reshape(1, -1)
    norm_len = norm_flat.shape[1]

    up_right = up_start.T
    emb_right = emb_start.T
    up_left = emb_left = None
    norm_total = None
    for step in range(up_gram_inv.shape[0]):
        parts = jnp.concatenate([left_t(up_field, up_right), left_t(emb_field, emb_right)], 1)
        sums = halving_sum(parts, ALL, replicas * tensors, dp_index * tensors + lax.axis_index("tensor"))
        up_left = normalized_t(sums[:, :up_rows], up_gram_inv[step], up_rows)
        emb_left = normalized_t(sums[:, up_rows:], emb_gram_inv[step], emb_rows)
        pieces = [right_t(up_field, up_left), right_t(emb_field, emb_left)]
        if step == 0:
            pad = -norm_len % up_right.shape[0]
            pieces.append(jnp.pad(norm_flat, ((0, 0), (0, pad))).reshape(up_right.shape[0], -1))
        sums = doubling_sum(jnp.concatenate(pieces, 1), "dp", replicas)
        up_right = sums[:, :up_cols]
        emb_right = sums[:, up_cols : up_cols + emb_cols]
        if step == 0:
            norm_total = sums[:, up_cols + emb_cols :].reshape(1, -1)[:, :norm_len]
            norm_total = norm_total.reshape(norm_grads.shape[1:])

    up_approx = outer_t(up_left, up_right) / replicas
    emb_approx = outer_t(emb_left, emb_right) / replicas
    up_error_new = (up_field - up_approx)[None]
    emb_error_new = (emb_field - emb_approx)[None]
    up_moment_all_new = BETA * up_moment_all + up_approx
    emb_moment_all_new = BETA * emb_moment_all + emb_approx
    up_step = (up_approx + BETA * up_moment_all_new).astype(jnp.bfloat16)
    emb_step = (emb_approx + BETA * emb_moment_all_new).astype(jnp.bfloat16)
    up_count = up_moment.shape[0]
    emb_count = emb_moment.shape[0]
    up_moment_new = lax.dynamic_slice_in_dim(up_moment_all_new, dp_index * up_count, up_count, 0)
    emb_moment_new = lax.dynamic_slice_in_dim(
        emb_moment_all_new, dp_index * emb_count, emb_count, 0
    )
    norm_mean = norm_total / replicas
    norm_moment_new = BETA * norm_moment + norm_mean
    norm_step = norm_mean + BETA * norm_moment_new
    return (
        up_error_new,
        emb_error_new,
        up_moment_new,
        emb_moment_new,
        up_step,
        emb_step,
        norm_moment_new,
        norm_step,
    )


def solution(mesh):
    return jax.shard_map(
        per_device,
        mesh=mesh,
        in_specs=(
            P("dp", None),
            P("dp", "tensor"),
            P("dp"),
            P("dp", "tensor"),
            P("dp", None, "tensor"),
            P("dp", None, "tensor"),
            P("dp", "tensor"),
            P("dp", "tensor"),
            P("tensor", None),
            P("tensor", None),
            P(),
            P(),
            P("dp", None, None),
            P(),
        ),
        out_specs=(
            P("dp", None, "tensor"),
            P("dp", None, "tensor"),
            P("dp", "tensor"),
            P("dp", "tensor"),
            P(None, "tensor"),
            P(None, "tensor"),
            P(),
            P(),
        ),
        check_vma=False,
    )
```

```python
import math

import jax
import jax.numpy as jnp
from jax import lax
from jax.sharding import PartitionSpec as P

BETA = 0.9
HIGHEST = lax.Precision.HIGHEST
HIGH = lax.Precision.HIGH
ALL = ("dp", "tensor")


def log2_of(n):
    bits = n.bit_length() - 1
    assert 1 << bits == n
    return bits


def partner(bit, n):
    return [(i, i ^ (1 << bit)) for i in range(n)]


def doubling_sum(x, axes, n):
    for bit in range(log2_of(n)):
        x = x + lax.ppermute(x, axes, partner(bit, n))
    return x


def split_axis(shape):
    rows, lanes = shape
    if lanes % 256 == 0:
        return 1
    if rows % 16 == 0:
        return 0
    return 1 if lanes % 2 == 0 else 0


def halving_sum(x, axes, n, index, middle=None):
    plan = []
    for bit in range(log2_of(n)):
        axis = split_axis(x.shape)
        half = x.shape[axis] // 2
        low = lax.slice_in_dim(x, 0, half, axis=axis)
        high = lax.slice_in_dim(x, half, 2 * half, axis=axis)
        upper = ((index >> bit) & 1) == 1
        keep = jnp.where(upper, high, low)
        send = jnp.where(upper, low, high)
        x = keep + lax.ppermute(send, axes, partner(bit, n))
        plan.append((bit, axis, upper))
    if middle is not None:
        x = middle(x)
    for bit, axis, upper in reversed(plan):
        got = lax.ppermute(x, axes, partner(bit, n))
        x = jnp.where(
            upper, jnp.concatenate([got, x], axis), jnp.concatenate([x, got], axis)
        )
    return x


def scale_of(left_sum_t, rows):
    return lax.rsqrt(jnp.mean(left_sum_t * left_sum_t) + 1e-06) / math.sqrt(rows)


def normalized_t(left_sum_t, gram, rows):
    out = lax.dot_general(gram, left_sum_t, (((0,), (0,)), ((), ())), precision=HIGH)
    return out * scale_of(left_sum_t, rows)


def left_t(field, right_t):
    return lax.dot_general(right_t, field, (((1,), (1,)), ((), ())), precision=HIGH)


def right_t(field, left_t_):
    return lax.dot_general(left_t_, field, (((1,), (0,)), ((), ())), precision=HIGH)


def split_bf16(x):
    high = lax.reduce_precision(x, exponent_bits=8, mantissa_bits=7)
    return high.astype(jnp.bfloat16), (x - high).astype(jnp.bfloat16)


def outer_t(left_t_, right_t_):
    left_high, left_low = split_bf16(left_t_)
    right_high, right_low = split_bf16(right_t_)
    lhs = jnp.concatenate([left_high, left_high, left_low], 0)
    rhs = jnp.concatenate([right_high, right_low, right_high], 0)
    return lax.dot_general(
        lhs, rhs, (((0,), (0,)), ((), ())), preferred_element_type=jnp.float32
    )


def per_device(
    up_inputs,
    up_grad_out,
    emb_ids,
    emb_grad_out,
    up_error,
    emb_error,
    up_moment,
    emb_moment,
    up_start,
    emb_start,
    up_gram_inv,
    emb_gram_inv,
    norm_grads,
    norm_moment,
):
    replicas = lax.axis_size("dp")
    tensors = lax.axis_size("tensor")
    dp_index = lax.axis_index("dp")

    up_moment_all = lax.all_gather(up_moment, "dp", axis=0, tiled=True)
    emb_moment_all = lax.all_gather(emb_moment, "dp", axis=0, tiled=True)

    up_field = (
        lax.dot_general(
            up_inputs, up_grad_out, (((0,), (0,)), ((), ())), preferred_element_type=jnp.float32
        )
        + up_error[0]
    )
    vocab = emb_error.shape[1]
    one_hot_cols = (
        lax.broadcasted_iota(jnp.int32, (vocab, emb_ids.shape[0]), 0) == emb_ids[None, :]
    ).astype(jnp.bfloat16)
    emb_terms = lax.dot_general(
        one_hot_cols, emb_grad_out, (((1,), (0,)), ((), ())), preferred_element_type=jnp.float32
    )
    emb_field = emb_terms + emb_error[0]
    up_rows, up_cols = up_field.shape
    emb_rows, emb_cols = emb_field.shape

    norm_flat = norm_grads[0].reshape(1, -1)
    norm_len = norm_flat.shape[1]

    up_right = up_start.T
    emb_right = emb_start.T
    up_left = emb_left = None
    norm_total = None
    for step in range(up_gram_inv.shape[0]):
        parts = jnp.concatenate([left_t(up_field, up_right), left_t(emb_field, emb_right)], 1)
        sums = halving_sum(parts, ALL, replicas * tensors, dp_index * tensors + lax.axis_index("tensor"))
        up_left = normalized_t(sums[:, :up_rows], up_gram_inv[step], up_rows)
        emb_left = normalized_t(sums[:, up_rows:], emb_gram_inv[step], emb_rows)
        pieces = [right_t(up_field, up_left), right_t(emb_field, emb_left)]
        if step == 0:
            pad = -norm_len % up_right.shape[0]
            pieces.append(jnp.pad(norm_flat, ((0, 0), (0, pad))).reshape(up_right.shape[0], -1))
        sums = doubling_sum(jnp.concatenate(pieces, 1), "dp", replicas)
        up_right = sums[:, :up_cols]
        emb_right = sums[:, up_cols : up_cols + emb_cols]
        if step == 0:
            norm_total = sums[:, up_cols + emb_cols :].reshape(1, -1)[:, :norm_len]
            norm_total = norm_total.reshape(norm_grads.shape[1:])

    up_approx = outer_t(up_left, up_right) / replicas
    emb_approx = outer_t(emb_left, emb_right) / replicas
    up_error_new = (up_field - up_approx)[None]
    emb_error_new = (emb_field - emb_approx)[None]
    up_moment_all_new = BETA * up_moment_all + up_approx
    emb_moment_all_new = BETA * emb_moment_all + emb_approx
    up_step = (up_approx + BETA * up_moment_all_new).astype(jnp.bfloat16)
    emb_step = (emb_approx + BETA * emb_moment_all_new).astype(jnp.bfloat16)
    up_count = up_moment.shape[0]
    emb_count = emb_moment.shape[0]
    up_moment_new = lax.dynamic_slice_in_dim(up_moment_all_new, dp_index * up_count, up_count, 0)
    emb_moment_new = lax.dynamic_slice_in_dim(
        emb_moment_all_new, dp_index * emb_count, emb_count, 0
    )
    norm_mean = norm_total / replicas
    norm_moment_new = BETA * norm_moment + norm_mean
    norm_step = norm_mean + BETA * norm_moment_new
    return (
        up_error_new,
        emb_error_new,
        up_moment_new,
        emb_moment_new,
        up_step,
        emb_step,
        norm_moment_new,
        norm_step,
    )


def solution(mesh):
    return jax.shard_map(
        per_device,
        mesh=mesh,
        in_specs=(
            P("dp", None),
            P("dp", "tensor"),
            P("dp"),
            P("dp", "tensor"),
            P("dp", None, "tensor"),
            P("dp", None, "tensor"),
            P("dp", "tensor"),
            P("dp", "tensor"),
            P("tensor", None),
            P("tensor", None),
            P(),
            P(),
            P("dp", None, None),
            P(),
        ),
        out_specs=(
            P("dp", None, "tensor"),
            P("dp", None, "tensor"),
            P("dp", "tensor"),
            P("dp", "tensor"),
            P(None, "tensor"),
            P(None, "tensor"),
            P(),
            P(),
        ),
        check_vma=False,
    )
```
